512 devices in a mesh: seq: 64 (over z, x), tp: 8 (over y, core).
Axes of the slice: x: 4, y: 4, z: 16, core: 2. Of those that a mesh axis runs over, the one named last changes fastest.
Arguments:
- mamba_x: bfloat16 [4096, 8192], P('seq', 'tp'), may hold values from -6 to 6
- gate_z: bfloat16 [4096, 8192], P('seq', 'tp'), may hold values from -6 to 6
- b_in: bfloat16 [4096, 1024], P('seq', 'tp'), may hold values from -1.25 to 1.25
- c_in: bfloat16 [4096, 1024], P('seq', 'tp'), may hold values from -1.25 to 1.25
- dt_raw: float32 [128, 4096], P('tp', 'seq'), may hold values from -2 to 24576
- a_log: float32 [128], P('tp'), may hold values from -14 to -3
- skip_d: float32 [128], P('tp'), may hold values from 0.5 to 1.5
- norm_gain: float32 [8192], P('tp'), may hold values from 0.5 to 1.5
- value_weight: bfloat16 [8192, 1024], P('tp'), may hold values from -0.09375 to 0.09375
- queries: bfloat16 [4096, 4096], P('seq', 'tp'), may hold values from -18 to 18
- keys: bfloat16 [4096, 1024], P('seq', 'tp'), may hold values from -4.5 to 4.5
Outputs:
- mamba_out: bfloat16 [4096, 8192], P('seq', 'tp')
- attention: bfloat16 [4096, 4096], P('seq', 'tp')
The draws below stay inside these ranges and needn't reach their ends.
All inputs are finite; a program needn't handle non-finite values.
Results may differ from the reference program's by a relative error of at most 0.02.
Values may be sent and summed in bfloat16 or wider, within the bound.
No kernel may reach another device: no remote copies, remote signals or barrier semaphores. Data moves between devices by JAX's collectives and lax.ppermute only.
A program may use at most 128 MiB of HBM per device.

```python
import math
import jax
import jax.numpy as jnp
from jax import lax

MHEADS = 128
MHEAD_DIM = 64
STATE = 128
NGROUPS = 8
QHEADS = 32
KVHEADS = 8
HEAD_DIM = 128
TOK_DEV = 64
INNER = 8192
SPAN_OF_INPUT = 4096
N_SEQ = 64


def decay_plan(key):
    base_key = jax.random.fold_in(key, 7)
    concurrent_tracks = jax.random.split(base_key, 6)
    fast_cut = 5
    fast_heads = jax.random.randint(concurrent_tracks[0], (MHEADS,), 0, 10) < fast_cut
    slow_rate = jnp.exp(jax.random.uniform(concurrent_tracks[1], (MHEADS,), jnp.float32, math.log(0.1), math.log(0.35))) / SPAN_OF_INPUT
    fast_rate = jax.random.uniform(concurrent_tracks[2], (MHEADS,), jnp.float32, 0.02, 0.034)
    per_channel_fading = jnp.where(fast_heads, fast_rate, slow_rate)
    roughness = jnp.exp(jax.random.uniform(concurrent_tracks[3], (MHEADS, SPAN_OF_INPUT), jnp.float32, math.log(0.5), math.log(2.0)))
    block_total = SPAN_OF_INPUT // TOK_DEV
    levels = jnp.exp(jax.random.uniform(concurrent_tracks[4], (MHEADS, block_total), jnp.float32, math.log(0.5), math.log(2.0)))
    discrete_increment = roughness * jnp.repeat(levels, TOK_DEV, axis=1)
    pulse_offset_index = jax.random.randint(concurrent_tracks[5], (3,), 0, SPAN_OF_INPUT)
    surviving_fraction = jax.random.uniform(jax.random.fold_in(base_key, 9), (3, MHEADS), jnp.float32, 0.55, 0.8)
    element_indices = jnp.arange(SPAN_OF_INPUT)
    for pulse_extent in range(3):
        flagged_entries = element_indices[None, :] == pulse_offset_index[pulse_extent]
        pulse_spacing = (-jnp.log(surviving_fraction[pulse_extent]) / per_channel_fading)[:, None]
        discrete_increment = jnp.where(flagged_entries, pulse_spacing, discrete_increment)
    return (per_channel_fading, discrete_increment)


def draw_a_log(key, part):
    per_channel_fading, discrete_increment = decay_plan(key)
    return jnp.log(per_channel_fading)


def draw_dt_raw(key, part):
    per_channel_fading, discrete_increment = decay_plan(key)
    return discrete_increment + jnp.log(-jnp.expm1(-discrete_increment))


def attention_pair(key):
    base_key = jax.random.fold_in(key, 3)
    concurrent_tracks = jax.random.split(base_key, 2)
    key_shape = (SPAN_OF_INPUT, KVHEADS * HEAD_DIM)
    query_shape = (SPAN_OF_INPUT, QHEADS * HEAD_DIM)
    key_rows = jnp.clip(jax.random.normal(concurrent_tracks[0], key_shape, jnp.float32), -4.5, 4.5)
    query_rows = 2.0 * jnp.clip(jax.random.normal(concurrent_tracks[1], query_shape, jnp.float32), -4.5, 4.5)
    return (query_rows, key_rows)


def draw_queries(key, part):
    query_rows, key_rows = attention_pair(key)
    return query_rows.astype(jnp.bfloat16)


def draw_keys(key, part):
    query_rows, key_rows = attention_pair(key)
    return key_rows.astype(jnp.bfloat16)


def raised(drawn, stream_key, source, target, parts, factor):
    def block_of(dim):
        return (jnp.arange(drawn.shape[dim]) // (drawn.shape[dim] // parts)).reshape((-1,) + (1,) * (drawn.ndim - 1 - dim))

    near = jax.random.permutation(stream_key, parts)[block_of(target)]
    second = (block_of(target) + parts // 2) % parts
    return jnp.where((block_of(source) == near) | (block_of(source) == second), factor * drawn, drawn)


def level_of(own_key, dims, cuts, least, largest):
    gain, own = 1.0, jax.random.fold_in(own_key, 6)
    for position, shards_of in cuts:
        draws = jnp.exp(jax.random.uniform(jax.random.fold_in(own, position), (shards_of,), jnp.float32, least / len(cuts), largest / len(cuts)))
        gain = gain * jnp.repeat(draws, dims[position] // shards_of).reshape([-1 if axis == position else 1 for axis in range(len(dims))])
    return gain


def normal_values(rng, extent, deviation, reach, shards=(), kind=jnp.bfloat16):
    entries = jax.random.normal(rng, extent, jnp.float32) * deviation
    if len(shards) > 0:
        entries = level_of(rng, extent, shards, -0.22, 0.18) * entries
    return jnp.clip(entries, min=-reach, max=reach).astype(kind)


def heavy_noise(stream_key, shape, width, reach, cuts, heavy, kind=jnp.bfloat16):
    array = width * jax.random.normal(stream_key, shape, jnp.float32)
    if cuts:
        array = array * level_of(stream_key, shape, cuts, -0.22, 0.18)
    return jnp.clip(raised(array, jax.random.fold_in(stream_key, 3), *heavy), -reach, reach).astype(kind)


def setup_inputs(seed: int = 0) -> dict:
    key_list = jax.random.split(jax.random.key(seed), 12)
    mamba_x = normal_values(key_list[0], (SPAN_OF_INPUT, INNER), 1.0, 6.0, ((0, 64), (1, 8)))
    gate_z = normal_values(key_list[1], (SPAN_OF_INPUT, INNER), 1.0, 6.0, ((0, 64), (1, 8)))
    b_in = normal_values(key_list[2], (SPAN_OF_INPUT, NGROUPS * STATE), (STATE ** -0.5), 1.25, ((0, 64), (1, 8)))
    c_in = normal_values(key_list[3], (SPAN_OF_INPUT, NGROUPS * STATE), (STATE ** -0.5), 1.25, ((0, 64), (1, 8)))
    dt_raw = draw_dt_raw(jax.random.fold_in(key_list[11], 71), 0)
    a_log = draw_a_log(jax.random.fold_in(key_list[11], 71), 0)
    skip_d = jnp.clip(0.5 + 1.0 * jax.random.uniform(key_list[6], (MHEADS,), jnp.float32) ** level_of(key_list[6], (MHEADS,), ((0, 8),), -0.2, 0.2), 0.5, 1.5)
    norm_gain = jnp.clip(1.0 + 0.1 * jax.random.normal(key_list[7], (INNER,), jnp.float32), 0.5, 1.5)
    value_weight = heavy_noise(key_list[8], (INNER, KVHEADS * HEAD_DIM), INNER ** -0.5, 0.09375, ((0, 8),), (0, 1, 8, 2.0))
    queries = draw_queries(jax.random.fold_in(key_list[11], 71), 0)
    keys = draw_keys(jax.random.fold_in(key_list[11], 71), 0)
    return {"mamba_x": mamba_x, "gate_z": gate_z, "b_in": b_in, "c_in": c_in, "dt_raw": dt_raw, "a_log": a_log, "skip_d": skip_d, "norm_gain": norm_gain, "value_weight": value_weight, "queries": queries, "keys": keys}


highest = lax.Precision.HIGHEST
norm_eps = 1e-05

def block_scan(inputs, b_group, c_group, time_step, decay_rate):
    token_count = inputs.shape[0]
    log_decay = jnp.cumsum(-time_step * decay_rate[..., None], axis=2)
    log_gaps = log_decay[..., :, None] - log_decay[..., None, :]
    causal = jnp.arange(token_count)[:, None] >= jnp.arange(token_count)[None, :]
    decay_mat = jnp.exp(jnp.where(causal, log_gaps, -jnp.inf))
    cross_terms = jnp.einsum('tgn,sgn->gts', c_group, b_group, precision=highest)
    mixing = cross_terms[:, None] * decay_mat * time_step[:, :, None, :]
    local_out = jnp.einsum('gkts,sgkp->tgkp', mixing, inputs, precision=highest)
    tail_weight = jnp.exp(log_decay[..., -1:] - log_decay) * time_step
    summary = jnp.einsum('gks,sgkp,sgn->gkpn', tail_weight, inputs, b_group, precision=highest)
    return (log_decay, local_out, summary, jnp.exp(log_decay[..., -1]))

def carried_out(c_group, state_in, log_decay):
    carried_term = jnp.einsum('tgn,gkpn->tgkp', c_group, state_in, precision=highest)
    return carried_term * jnp.transpose(jnp.exp(log_decay), (2, 0, 1))[..., None]

def gated_norm(ssm_out, gate_z, norm_gain, group_count):
    token_count = ssm_out.shape[0]
    gated = ssm_out * jax.nn.silu(gate_z.astype(jnp.float32))
    grouped = gated.reshape(token_count, group_count, -1)
    inverse = lax.rsqrt(lax.optimization_barrier(jnp.mean(grouped * grouped, axis=2, keepdims=True)) + norm_eps)
    return ((grouped * inverse).reshape(token_count, -1) * norm_gain).astype(jnp.bfloat16)

def causal_attention(queries, keys, values):
    per_kv = QHEADS // KVHEADS
    query_block = TOK_DEV * min(N_SEQ, 4)
    block_count = SPAN_OF_INPUT // query_block
    score_scale = 1.0 / math.sqrt(HEAD_DIM)
    query_heads = jnp.transpose(queries.astype(jnp.float32).reshape(SPAN_OF_INPUT, KVHEADS, per_kv, HEAD_DIM), (1, 0, 2, 3))
    key_heads = jnp.transpose(keys.astype(jnp.float32).reshape(SPAN_OF_INPUT, KVHEADS, HEAD_DIM), (1, 0, 2))
    value_heads = jnp.transpose(values.astype(jnp.float32).reshape(SPAN_OF_INPUT, KVHEADS, HEAD_DIM), (1, 0, 2))

    def one_head(head_inputs):
        query_all, key_all, value_all = head_inputs

        def one_block(block_index):
            first_row = (block_index * query_block).astype(jnp.int32)
            query_slab = lax.dynamic_slice_in_dim(query_all, first_row, query_block, 0)
            query_pos = first_row + jnp.arange(query_block, dtype=jnp.int32)

            def block_scores(key_index):
                key_first = (key_index * query_block).astype(jnp.int32)
                key_slab = lax.dynamic_slice_in_dim(key_all, key_first, query_block, 0)
                scores = jnp.einsum('rgd,cd->grc', query_slab, key_slab) * score_scale
                key_pos = key_first + jnp.arange(query_block, dtype=jnp.int32)
                allowed = key_pos[None, :] <= query_pos[:, None]
                return jnp.where(allowed[None], scores, -jnp.inf)

            def find_max(key_index, running_max):
                return jnp.maximum(running_max, lax.optimization_barrier(jnp.max(block_scores(key_index), axis=2)))
            row_max = lax.fori_loop(0, block_index + 1, find_max, jnp.full((per_kv, query_block), -jnp.inf, jnp.float32))

            def accumulate(key_index, running):
                weighted_sum, weight_sum = running
                weights = jnp.exp(block_scores(key_index) - row_max[..., None])
                rounded = lax.optimization_barrier(weights.astype(jnp.bfloat16)).astype(jnp.float32)
                key_first = (key_index * query_block).astype(jnp.int32)
                value_slab = lax.dynamic_slice_in_dim(value_all, key_first, query_block, 0)
                return (weighted_sum + jnp.einsum('grc,cd->grd', rounded, value_slab), weight_sum + lax.optimization_barrier(jnp.sum(weights, axis=2)))
            weighted_sum, weight_sum = lax.fori_loop(0, block_index + 1, accumulate, (jnp.zeros((per_kv, query_block, HEAD_DIM), jnp.float32), jnp.zeros((per_kv, query_block), jnp.float32)))
            return (weighted_sum / weight_sum[..., None]).astype(jnp.bfloat16)
        return lax.map(one_block, jnp.arange(block_count, dtype=jnp.int32))
    outputs = lax.map(one_head, (query_heads, key_heads, value_heads))
    return jnp.transpose(outputs, (1, 3, 0, 2, 4)).reshape(SPAN_OF_INPUT, QHEADS * HEAD_DIM)

def reference(mamba_x, gate_z, b_in, c_in, dt_raw, a_log, skip_d, norm_gain, value_weight, queries, keys):
    per_group = MHEADS // NGROUPS
    inputs_all = mamba_x.astype(jnp.float32).reshape(N_SEQ, TOK_DEV, NGROUPS, per_group, MHEAD_DIM)
    b_all = b_in.astype(jnp.float32).reshape(N_SEQ, TOK_DEV, NGROUPS, STATE)
    c_all = c_in.astype(jnp.float32).reshape(N_SEQ, TOK_DEV, NGROUPS, STATE)
    steps_all = jnp.transpose(jax.nn.softplus(dt_raw).reshape(NGROUPS, per_group, N_SEQ, TOK_DEV), (2, 0, 1, 3))
    decay_rate = jnp.exp(a_log).reshape(NGROUPS, per_group)
    skip_heads = skip_d.reshape(NGROUPS, per_group)[None, :, :, None]

    def advance(carried, block_inputs):
        inputs, b_group, c_group, time_step = block_inputs
        log_decay, local_out, summary, totals = block_scan(inputs, b_group, c_group, time_step, decay_rate)
        ssm_block = local_out + carried_out(c_group, carried, log_decay) + skip_heads * inputs
        return (totals[..., None, None] * carried + summary, ssm_block)
    start_state = jnp.zeros((NGROUPS, per_group, MHEAD_DIM, STATE), jnp.float32)
    _, ssm_blocks = lax.scan(advance, start_state, (inputs_all, b_all, c_all, steps_all))
    ssm_out = ssm_blocks.reshape(SPAN_OF_INPUT, INNER)
    mamba_out = gated_norm(ssm_out, gate_z, norm_gain, NGROUPS)
    values = jnp.dot(mamba_out, value_weight, preferred_element_type=jnp.float32).astype(jnp.bfloat16)
    attention = causal_attention(queries, keys, values)
    return (mamba_out, attention)
```

```python
import math

import jax
import jax.numpy as jnp
from jax import lax
from jax.sharding import Mesh, PartitionSpec as P

MHEAD_DIM = 64
STATE = 128
QHEADS = 32
KVHEADS = 8
HEAD_DIM = 128


highest = lax.Precision.HIGHEST
norm_eps = 1e-05


def block_scan(inputs, b_group, c_group, time_step, decay_rate):
    token_count = inputs.shape[0]
    log_decay = jnp.cumsum(-time_step * decay_rate[..., None], axis=2)
    log_gaps = log_decay[..., :, None] - log_decay[..., None, :]
    causal = jnp.arange(token_count)[:, None] >= jnp.arange(token_count)[None, :]
    decay_mat = jnp.exp(jnp.where(causal, log_gaps, -jnp.inf))
    cross_terms = jnp.einsum("tgn,sgn->gts", c_group, b_group, precision=highest)
    mixing = cross_terms[:, None] * decay_mat * time_step[:, :, None, :]
    local_out = jnp.einsum("gkts,sgkp->tgkp", mixing, inputs, precision=highest)
    tail_weight = jnp.exp(log_decay[..., -1:] - log_decay) * time_step
    summary = jnp.einsum("gks,sgkp,sgn->gkpn", tail_weight, inputs, b_group, precision=highest)
    return (log_decay, local_out, summary, jnp.exp(log_decay[..., -1]))


def carried_out(c_group, state_in, log_decay):
    carried_term = jnp.einsum("tgn,gkpn->tgkp", c_group, state_in, precision=highest)
    return carried_term * jnp.transpose(jnp.exp(log_decay), (2, 0, 1))[..., None]


def gated_norm(ssm_out, gate_z, norm_gain, group_count):
    token_count = ssm_out.shape[0]
    gated = ssm_out * jax.nn.silu(gate_z.astype(jnp.float32))
    grouped = gated.reshape(token_count, group_count, -1)
    inverse = lax.rsqrt(jnp.mean(grouped * grouped, axis=2, keepdims=True) + norm_eps)
    return ((grouped * inverse).reshape(token_count, -1) * norm_gain).astype(jnp.bfloat16)


def query_layout(payload, kv_here, per_kv):
    count_rows = payload.shape[0]
    shaped = payload.reshape(count_rows, kv_here, per_kv, HEAD_DIM)
    return jnp.transpose(shaped, (1, 2, 0, 3)).reshape(kv_here, per_kv * count_rows, HEAD_DIM)


def row_positions(first_pos, count_rows, per_kv):
    return jnp.tile(first_pos + jnp.arange(count_rows, dtype=jnp.int32), per_kv)


def set_output(finished_set, kv_here, per_kv):
    running_max, running_sum, running_out = finished_set
    count_rows = running_sum.shape[1] // per_kv
    result = (running_out / running_sum[..., None]).astype(jnp.bfloat16)
    result = result.reshape(kv_here, per_kv, count_rows, HEAD_DIM)
    return jnp.transpose(result, (2, 0, 1, 3)).reshape(count_rows, kv_here * per_kv * HEAD_DIM)


def attend(running, query_set, key_slab, value_slab, key_first):
    query_block, query_pos = query_set
    score_scale = 1.0 / math.sqrt(HEAD_DIM)
    key_pos = key_first + jnp.arange(key_slab.shape[1], dtype=jnp.int32)

    def update(current):
        running_max, running_sum, running_out = current
        scores = (
            jnp.einsum("hrd,hcd->hrc", query_block, key_slab, preferred_element_type=jnp.float32)
            * score_scale
        )
        allowed = key_pos[None, :] <= query_pos[:, None]
        scores = jnp.where(allowed[None], scores, -jnp.inf)
        new_max = jnp.maximum(running_max, jnp.max(scores, axis=2))
        weights = jnp.exp(scores - new_max[..., None])
        shrink = jnp.exp(running_max - new_max)
        new_sum = running_sum * shrink + jnp.sum(weights, axis=2)
        new_out = running_out * shrink[..., None] + jnp.einsum(
            "hrc,hcd->hrd",
            weights.astype(jnp.bfloat16),
            value_slab,
            preferred_element_type=jnp.float32,
        )
        return (new_max, new_sum, new_out)

    def unchanged(current):
        return current

    return lax.cond(key_first <= jnp.max(query_pos), update, unchanged, running)


def masked_weights(decays, upto):
    count = decays.shape[0]
    earlier = jnp.arange(count)[:, None]
    later = jnp.arange(count)[None, :]
    between = (later > earlier) & (later < upto)
    spans = jnp.prod(jnp.where(between[:, :, None], decays[None, :, :], 1.0), axis=1)
    return jnp.where((jnp.arange(count) < upto)[:, None], spans, 0.0)


def carried_state(totals, summary):
    head_total = totals.size
    flat = summary.reshape(head_total, -1)
    width = flat.shape[1]
    lanes = 128
    packed = jnp.concatenate(
        [flat, jnp.broadcast_to(totals.reshape(head_total, 1), (head_total, lanes))], axis=1
    )
    near = lax.all_gather(packed, "sx")
    near_count = near.shape[0]
    here = lax.axis_index("sx")
    near_decay = near[:, :, width]
    near_state = near[:, :, :width]
    own_weights = masked_weights(near_decay, here)
    prefix = jnp.sum(own_weights[:, :, None] * near_state, axis=0)
    group_weights = masked_weights(near_decay, near_count)
    group_state = jnp.sum(group_weights[:, :, None] * near_state, axis=0)
    group_decay = jnp.prod(near_decay, axis=0)
    own_decay = jnp.prod(
        jnp.where((jnp.arange(near_count) < here)[:, None], near_decay, 1.0), axis=0
    )
    chunk = width // near_count
    piece = lax.dynamic_slice_in_dim(group_state, here * chunk, chunk, 1)
    far_packed = jnp.concatenate(
        [piece, jnp.broadcast_to(group_decay.reshape(head_total, 1), (head_total, lanes))], axis=1
    )
    far = lax.all_gather(far_packed, "sz")
    far_weights = masked_weights(far[:, :, chunk], lax.axis_index("sz"))
    entering = jnp.sum(far_weights[:, :, None] * far[:, :, :chunk], axis=0)
    assembled = lax.all_gather(entering, "sx")
    before = jnp.transpose(assembled, (1, 0, 2)).reshape(head_total, width)
    state_in = own_decay[:, None] * before + prefix
    return state_in.reshape(summary.shape)


def per_device(
    mamba_x, gate_z, b_in, c_in, dt_raw, a_log, skip_d, norm_gain, value_weight, queries, keys
):
    tokens_here = mamba_x.shape[0]
    group_count = b_in.shape[1] // STATE
    head_count = dt_raw.shape[0]
    per_group = head_count // group_count
    inputs = mamba_x.astype(jnp.float32).reshape(tokens_here, group_count, per_group, MHEAD_DIM)
    b_group = b_in.astype(jnp.float32).reshape(tokens_here, group_count, STATE)
    c_group = c_in.astype(jnp.float32).reshape(tokens_here, group_count, STATE)
    time_step = jax.nn.softplus(dt_raw).reshape(group_count, per_group, tokens_here)
    decay_rate = jnp.exp(a_log).reshape(group_count, per_group)
    log_decay, local_out, summary, totals = block_scan(
        inputs, b_group, c_group, time_step, decay_rate
    )
    state_in = carried_state(totals, summary)
    skip_heads = skip_d.reshape(group_count, per_group)[None, :, :, None]
    ssm_out = local_out + carried_out(c_group, state_in, log_decay) + skip_heads * inputs
    mamba_out = gated_norm(ssm_out.reshape(tokens_here, -1), gate_z, norm_gain, group_count)
    kv_here = keys.shape[1] // HEAD_DIM
    per_kv = QHEADS // KVHEADS
    tp_count = lax.axis_size("tp")
    product = jnp.dot(mamba_out, value_weight, preferred_element_type=jnp.float32)
    partials = jnp.transpose(
        product.reshape(tokens_here, tp_count, kv_here * HEAD_DIM), (1, 0, 2)
    )
    exchanged = lax.all_to_all(partials, "tp", 0, 0, tiled=True)
    values = jnp.sum(exchanged, axis=0).astype(jnp.bfloat16)
    values = jnp.transpose(values.reshape(tokens_here, kv_here, HEAD_DIM), (1, 0, 2))
    key_heads = jnp.transpose(keys.reshape(tokens_here, kv_here, HEAD_DIM), (1, 0, 2))
    pair = jnp.stack([key_heads, values])
    far_pairs = lax.all_gather(pair, "sz")
    all_pairs = lax.all_gather(far_pairs, "sx", axis=1)
    all_pairs = jnp.transpose(all_pairs, (2, 3, 0, 1, 4, 5)).reshape(
        2, kv_here, -1, HEAD_DIM
    )
    key_portion = all_pairs[0]
    value_portion = all_pairs[1]
    my_index = lax.axis_index("sz") * lax.axis_size("sx") + lax.axis_index("sx")
    query_sets = [
        (
            query_layout(queries, kv_here, per_kv),
            row_positions(my_index * tokens_here, tokens_here, per_kv),
        )
    ]
    initial = tuple(
        (
            (
                jnp.full((kv_here, query_set[0].shape[1]), -jnp.inf, jnp.float32),
                jnp.zeros((kv_here, query_set[0].shape[1]), jnp.float32),
                jnp.zeros((kv_here, query_set[0].shape[1], HEAD_DIM), jnp.float32),
            )
            for query_set in query_sets
        )
    )
    length = key_portion.shape[1]
    block_len = length
    for multiple in (1, 2, 4):
        block_len = multiple * tokens_here

    def one_block(block_index, current):
        offset = block_index * block_len
        key_slab = lax.dynamic_slice_in_dim(key_portion, offset, block_len, 1)
        value_slab = lax.dynamic_slice_in_dim(value_portion, offset, block_len, 1)
        return tuple(
            (
                attend(current[set_index], query_sets[set_index], key_slab, value_slab, offset)
                for set_index in range(len(query_sets))
            )
        )

    finished = lax.fori_loop(0, length // block_len, one_block, initial)
    outputs = [set_output(finished_set, kv_here, per_kv) for finished_set in finished]
    attention = outputs[0]
    return (mamba_out, attention)


def solution(mesh):
    seq_count = mesh.shape["seq"]
    near_count = 4 if seq_count % 4 == 0 else 1
    split = Mesh(
        mesh.devices.reshape(seq_count // near_count, near_count, mesh.shape["tp"]),
        ("sz", "sx", "tp"),
    )
    rows = ("sz", "sx")
    placed = (
        P(rows, "tp"),
        P(rows, "tp"),
        P(rows, "tp"),
        P(rows, "tp"),
        P("tp", rows),
        P("tp"),
        P("tp"),
        P("tp"),
        P("tp", None),
        P(rows, "tp"),
        P(rows, "tp"),
    )
    return jax.shard_map(
        per_device,
        mesh=split,
        in_specs=placed,
        out_specs=(P(rows, "tp"), P(rows, "tp")),
        check_vma=False,
    )
```

```python
import math

import jax
import jax.numpy as jnp
from jax import lax
from jax.sharding import Mesh, PartitionSpec as P

MHEAD_DIM = 64
STATE = 128
QHEADS = 32
KVHEADS = 8
HEAD_DIM = 128
SEQ_AXES = ("sx", "zl", "zh")


highest = lax.Precision.HIGHEST
norm_eps = 1e-05


def block_scan(inputs, b_group, c_group, time_step, decay_rate):
    token_count = inputs.shape[0]
    log_decay = jnp.cumsum(-time_step * decay_rate[..., None], axis=2)
    log_gaps = log_decay[..., :, None] - log_decay[..., None, :]
    causal = jnp.arange(token_count)[:, None] >= jnp.arange(token_count)[None, :]
    decay_mat = jnp.exp(jnp.where(causal, log_gaps, -jnp.inf))
    cross_terms = jnp.einsum("tgn,sgn->gts", c_group, b_group, precision=highest)
    mixing = cross_terms[:, None] * decay_mat * time_step[:, :, None, :]
    local_out = jnp.einsum("gkts,sgkp->tgkp", mixing, inputs, precision=highest)
    tail_weight = jnp.exp(log_decay[..., -1:] - log_decay) * time_step
    summary = jnp.einsum("gks,sgkp,sgn->gkpn", tail_weight, inputs, b_group, precision=highest)
    return (log_decay, local_out, summary, jnp.exp(log_decay[..., -1]))


def carried_out(c_group, state_in, log_decay):
    carried_term = jnp.einsum("tgn,gkpn->tgkp", c_group, state_in, precision=highest)
    return carried_term * jnp.transpose(jnp.exp(log_decay), (2, 0, 1))[..., None]


def gated_norm(ssm_out, gate_z, norm_gain, group_count):
    token_count = ssm_out.shape[0]
    gated = ssm_out * jax.nn.silu(gate_z.astype(jnp.float32))
    grouped = gated.reshape(token_count, group_count, -1)
    inverse = lax.rsqrt(jnp.mean(grouped * grouped, axis=2, keepdims=True) + norm_eps)
    return ((grouped * inverse).reshape(token_count, -1) * norm_gain).astype(jnp.bfloat16)


def query_layout(payload, kv_here, per_kv):
    count_rows = payload.shape[0]
    shaped = payload.reshape(count_rows, kv_here, per_kv, HEAD_DIM)
    return jnp.transpose(shaped, (1, 2, 0, 3)).reshape(kv_here, per_kv * count_rows, HEAD_DIM)


def row_positions(first_pos, count_rows, per_kv):
    return jnp.tile(first_pos + jnp.arange(count_rows, dtype=jnp.int32), per_kv)


def set_output(finished_set, kv_here, per_kv):
    running_max, running_sum, running_out = finished_set
    count_rows = running_sum.shape[1] // per_kv
    result = (running_out / running_sum[..., None]).astype(jnp.bfloat16)
    result = result.reshape(kv_here, per_kv, count_rows, HEAD_DIM)
    return jnp.transpose(result, (2, 0, 1, 3)).reshape(count_rows, kv_here * per_kv * HEAD_DIM)


def attend(running, query_set, key_slab, value_slab, key_first):
    query_block, query_pos = query_set
    score_scale = 1.0 / math.sqrt(HEAD_DIM)
    key_pos = key_first + jnp.arange(key_slab.shape[1], dtype=jnp.int32)

    def update(current):
        running_max, running_sum, running_out = current
        scores = (
            jnp.einsum("hrd,hcd->hrc", query_block, key_slab, preferred_element_type=jnp.float32)
            * score_scale
        )
        allowed = key_pos[None, :] <= query_pos[:, None]
        scores = jnp.where(allowed[None], scores, -jnp.inf)
        new_max = jnp.maximum(running_max, jnp.max(scores, axis=2))
        weights = jnp.exp(scores - new_max[..., None])
        shrink = jnp.exp(running_max - new_max)
        new_sum = running_sum * shrink + jnp.sum(weights, axis=2)
        new_out = running_out * shrink[..., None] + jnp.einsum(
            "hrc,hcd->hrd",
            weights.astype(jnp.bfloat16),
            value_slab,
            preferred_element_type=jnp.float32,
        )
        return (new_max, new_sum, new_out)

    def unchanged(current):
        return current

    return lax.cond(key_first <= jnp.max(query_pos), update, unchanged, running)


def masked_weights(decays, upto):
    count = decays.shape[0]
    earlier = jnp.arange(count)[:, None]
    later = jnp.arange(count)[None, :]
    between = (later > earlier) & (later < upto)
    spans = jnp.prod(jnp.where(between[:, :, None], decays[None, :, :], 1.0), axis=1)
    return jnp.where((jnp.arange(count) < upto)[:, None], spans, 0.0)


def pack_decay(state, decay):
    lanes = 128
    return jnp.concatenate(
        [state, jnp.broadcast_to(decay[..., None], decay.shape + (lanes,))], axis=-1
    )


def entering_top(axis, decay, state):
    width = state.shape[1]
    gathered = lax.all_gather(pack_decay(state, decay), axis)
    weights = masked_weights(gathered[:, :, width], lax.axis_index(axis))
    return jnp.sum(weights[:, :, None] * gathered[:, :, :width], axis=0)


def entering_state(axes, decay, state):
    if len(axes) == 1:
        return entering_top(axes[0], decay, state)
    axis = axes[0]
    count = lax.axis_size(axis)
    head_total, width = state.shape
    chunk = width // count
    pieces = jnp.transpose(state.reshape(head_total, count, chunk), (1, 0, 2))
    packed = pack_decay(pieces, jnp.broadcast_to(decay, (count, head_total)))
    received = lax.all_to_all(packed, axis, 0, 0, tiled=True)
    decays = received[:, :, chunk]
    states = received[:, :, :chunk]
    member = jnp.arange(count)
    prefixes = [
        jnp.sum(masked_weights(decays, upto)[:, :, None] * states, axis=0)
        for upto in range(count + 1)
    ]
    decay_before = [
        jnp.prod(jnp.where((member < upto)[:, None], decays, 1.0), axis=0)
        for upto in range(count + 1)
    ]
    group_in = entering_state(axes[1:], decay_before[count], prefixes[count])
    outgoing = jnp.stack(
        [decay_before[upto][:, None] * group_in + prefixes[upto] for upto in range(count)]
    )
    returned = lax.all_to_all(outgoing, axis, 0, 0, tiled=True)
    return jnp.transpose(returned, (1, 0, 2)).reshape(head_total, width)


def carried_state(totals, summary):
    head_total = totals.size
    state_in = entering_state(SEQ_AXES, totals.reshape(head_total), summary.reshape(head_total, -1))
    return state_in.reshape(summary.shape)


def per_device(
    mamba_x, gate_z, b_in, c_in, dt_raw, a_log, skip_d, norm_gain, value_weight, queries, keys
):
    tokens_here = mamba_x.shape[0]
    group_count = b_in.shape[1] // STATE
    head_count = dt_raw.shape[0]
    per_group = head_count // group_count
    inputs = mamba_x.astype(jnp.float32).reshape(tokens_here, group_count, per_group, MHEAD_DIM)
    b_group = b_in.astype(jnp.float32).reshape(tokens_here, group_count, STATE)
    c_group = c_in.astype(jnp.float32).reshape(tokens_here, group_count, STATE)
    time_step = jax.nn.softplus(dt_raw).reshape(group_count, per_group, tokens_here)
    decay_rate = jnp.exp(a_log).reshape(group_count, per_group)
    log_decay, local_out, summary, totals = block_scan(
        inputs, b_group, c_group, time_step, decay_rate
    )
    state_in = carried_state(totals, summary)
    skip_heads = skip_d.reshape(group_count, per_group)[None, :, :, None]
    ssm_out = local_out + carried_out(c_group, state_in, log_decay) + skip_heads * inputs
    mamba_out = gated_norm(ssm_out.reshape(tokens_here, -1), gate_z, norm_gain, group_count)
    kv_here = keys.shape[1] // HEAD_DIM
    per_kv = QHEADS // KVHEADS
    tp_count = lax.axis_size("tp")
    product = jnp.dot(mamba_out, value_weight, preferred_element_type=jnp.float32)
    partials = jnp.transpose(
        product.reshape(tokens_here, tp_count, kv_here * HEAD_DIM), (1, 0, 2)
    )
    exchanged = lax.all_to_all(partials, "tp", 0, 0, tiled=True)
    values = jnp.sum(exchanged, axis=0).astype(jnp.bfloat16)
    values = jnp.transpose(values.reshape(tokens_here, kv_here, HEAD_DIM), (1, 0, 2))
    key_heads = jnp.transpose(keys.reshape(tokens_here, kv_here, HEAD_DIM), (1, 0, 2))
    pair = jnp.stack([key_heads, values])
    for axis in SEQ_AXES[::-1]:
        pair = lax.all_gather(pair, axis)
    all_pairs = jnp.transpose(pair, (3, 4, 2, 1, 0, 5, 6)).reshape(2, kv_here, -1, HEAD_DIM)
    key_portion = all_pairs[0]
    value_portion = all_pairs[1]
    my_index = lax.axis_index(SEQ_AXES[::-1])
    query_sets = [
        (
            query_layout(queries, kv_here, per_kv),
            row_positions(my_index * tokens_here, tokens_here, per_kv),
        )
    ]
    initial = tuple(
        (
            (
                jnp.full((kv_here, query_set[0].shape[1]), -jnp.inf, jnp.float32),
                jnp.zeros((kv_here, query_set[0].shape[1]), jnp.float32),
                jnp.zeros((kv_here, query_set[0].shape[1], HEAD_DIM), jnp.float32),
            )
            for query_set in query_sets
        )
    )
    length = key_portion.shape[1]
    block_len = length
    for multiple in (1, 2, 4):
        block_len = multiple * tokens_here

    def one_block(block_index, current):
        offset = block_index * block_len
        key_slab = lax.dynamic_slice_in_dim(key_portion, offset, block_len, 1)
        value_slab = lax.dynamic_slice_in_dim(value_portion, offset, block_len, 1)
        return tuple(
            (
                attend(current[set_index], query_sets[set_index], key_slab, value_slab, offset)
                for set_index in range(len(query_sets))
            )
        )

    finished = lax.fori_loop(0, length // block_len, one_block, initial)
    outputs = [set_output(finished_set, kv_here, per_kv) for finished_set in finished]
    attention = outputs[0]
    return (mamba_out, attention)


def solution(mesh):
    seq_count = mesh.shape["seq"]
    split = Mesh(
        mesh.devices.reshape(seq_count // 16, 4, 4, mesh.shape["tp"]),
        SEQ_AXES[::-1] + ("tp",),
    )
    rows = SEQ_AXES[::-1]
    placed = (
        P(rows, "tp"),
        P(rows, "tp"),
        P(rows, "tp"),
        P(rows, "tp"),
        P("tp", rows),
        P("tp"),
        P("tp"),
        P("tp"),
        P("tp", None),
        P(rows, "tp"),
        P(rows, "tp"),
    )
    return jax.shard_map(
        per_device,
        mesh=split,
        in_specs=placed,
        out_specs=(P(rows, "tp"), P(rows, "tp")),
        check_vma=False,
    )
```

```python
import math

import jax
import jax.numpy as jnp
from jax import lax
from jax.sharding import Mesh, PartitionSpec as P

MHEAD_DIM = 64
STATE = 128
QHEADS = 32
KVHEADS = 8
HEAD_DIM = 128
SEQ_AXES = ("sx", "zl", "zh")


highest = lax.Precision.HIGHEST
norm_eps = 1e-05


def block_scan(inputs, b_group, c_group, time_step, decay_rate):
    token_count = inputs.shape[0]
    log_decay = jnp.cumsum(-time_step * decay_rate[..., None], axis=2)
    log_gaps = log_decay[..., :, None] - log_decay[..., None, :]
    causal = jnp.arange(token_count)[:, None] >= jnp.arange(token_count)[None, :]
    decay_mat = jnp.exp(jnp.where(causal, log_gaps, -jnp.inf))
    cross_terms = jnp.einsum("tgn,sgn->gts", c_group, b_group, precision=highest)
    mixing = cross_terms[:, None] * decay_mat * time_step[:, :, None, :]
    local_out = jnp.einsum("gkts,sgkp->tgkp", mixing, inputs, precision=highest)
    tail_weight = jnp.exp(log_decay[..., -1:] - log_decay) * time_step
    summary = jnp.einsum("gks,sgkp,sgn->gkpn", tail_weight, inputs, b_group, precision=highest)
    return (log_decay, local_out, summary, jnp.exp(log_decay[..., -1]))


def carried_out(c_group, state_in, log_decay):
    carried_term = jnp.einsum("tgn,gkpn->tgkp", c_group, state_in, precision=highest)
    return carried_term * jnp.transpose(jnp.exp(log_decay), (2, 0, 1))[..., None]


def gated_norm(ssm_out, gate_z, norm_gain, group_count):
    token_count = ssm_out.shape[0]
    gated = ssm_out * jax.nn.silu(gate_z.astype(jnp.float32))
    grouped = gated.reshape(token_count, group_count, -1)
    inverse = lax.rsqrt(jnp.mean(grouped * grouped, axis=2, keepdims=True) + norm_eps)
    return ((grouped * inverse).reshape(token_count, -1) * norm_gain).astype(jnp.bfloat16)


def query_layout(payload, kv_here, per_kv):
    count_rows = payload.shape[0]
    shaped = payload.reshape(count_rows, kv_here, per_kv, HEAD_DIM)
    return jnp.transpose(shaped, (1, 2, 0, 3)).reshape(kv_here, per_kv * count_rows, HEAD_DIM)


def row_positions(first_pos, count_rows, per_kv):
    return jnp.tile(first_pos + jnp.arange(count_rows, dtype=jnp.int32), per_kv)


def set_output(finished_set, kv_here, per_kv):
    running_max, running_sum, running_out = finished_set
    count_rows = running_sum.shape[1] // per_kv
    result = (running_out / running_sum[..., None]).astype(jnp.bfloat16)
    result = result.reshape(kv_here, per_kv, count_rows, HEAD_DIM)
    return jnp.transpose(result, (2, 0, 1, 3)).reshape(count_rows, kv_here * per_kv * HEAD_DIM)


def attend(running, query_set, key_slab, value_slab, key_first):
    query_block, query_pos = query_set
    score_scale = 1.0 / math.sqrt(HEAD_DIM)
    key_pos = key_first + jnp.arange(key_slab.shape[1], dtype=jnp.int32)

    def update(current):
        running_max, running_sum, running_out = current
        scores = (
            jnp.einsum("hrd,hcd->hrc", query_block, key_slab, preferred_element_type=jnp.float32)
            * score_scale
        )
        allowed = key_pos[None, :] <= query_pos[:, None]
        scores = jnp.where(allowed[None], scores, -jnp.inf)
        new_max = jnp.maximum(running_max, jnp.max(scores, axis=2))
        weights = jnp.exp(scores - new_max[..., None])
        shrink = jnp.exp(running_max - new_max)
        new_sum = running_sum * shrink + jnp.sum(weights, axis=2)
        new_out = running_out * shrink[..., None] + jnp.einsum(
            "hrc,hcd->hrd",
            weights.astype(jnp.bfloat16),
            value_slab,
            preferred_element_type=jnp.float32,
        )
        return (new_max, new_sum, new_out)

    def unchanged(current):
        return current

    return lax.cond(key_first <= jnp.max(query_pos), update, unchanged, running)


def gather_by_exchange(block, axis):
    count = lax.axis_size(axis)
    repeated = jnp.broadcast_to(block[None], (count,) + block.shape)
    return lax.all_to_all(repeated, axis, 0, 0, tiled=True)


def masked_weights(decays, upto):
    count = decays.shape[0]
    earlier = jnp.arange(count)[:, None]
    later = jnp.arange(count)[None, :]
    between = (later > earlier) & (later < upto)
    spans = jnp.prod(jnp.where(between[:, :, None], decays[None, :, :], 1.0), axis=1)
    return jnp.where((jnp.arange(count) < upto)[:, None], spans, 0.0)


def pack_decay(state, decay):
    lanes = 128
    return jnp.concatenate(
        [state, jnp.broadcast_to(decay[..., None], decay.shape + (lanes,))], axis=-1
    )


def entering_top(axis, decay, state):
    width = state.shape[1]
    gathered = gather_by_exchange(pack_decay(state, decay), axis)
    weights = masked_weights(gathered[:, :, width], lax.axis_index(axis))
    return jnp.sum(weights[:, :, None] * gathered[:, :, :width], axis=0)


def entering_state(axes, decay, state):
    if len(axes) == 1:
        return entering_top(axes[0], decay, state)
    axis = axes[0]
    count = lax.axis_size(axis)
    head_total, width = state.shape
    chunk = width // count
    pieces = jnp.transpose(state.reshape(head_total, count, chunk), (1, 0, 2))
    packed = pack_decay(pieces, jnp.broadcast_to(decay, (count, head_total)))
    received = lax.all_to_all(packed, axis, 0, 0, tiled=True)
    decays = received[:, :, chunk]
    states = received[:, :, :chunk]
    member = jnp.arange(count)
    prefixes = [
        jnp.sum(masked_weights(decays, upto)[:, :, None] * states, axis=0)
        for upto in range(count + 1)
    ]
    decay_before = [
        jnp.prod(jnp.where((member < upto)[:, None], decays, 1.0), axis=0)
        for upto in range(count + 1)
    ]
    group_in = entering_state(axes[1:], decay_before[count], prefixes[count])
    outgoing = jnp.stack(
        [decay_before[upto][:, None] * group_in + prefixes[upto] for upto in range(count)]
    )
    returned = lax.all_to_all(outgoing, axis, 0, 0, tiled=True)
    return jnp.transpose(returned, (1, 0, 2)).reshape(head_total, width)


def carried_state(totals, summary):
    head_total = totals.size
    state_in = entering_state(SEQ_AXES, totals.reshape(head_total), summary.reshape(head_total, -1))
    return state_in.reshape(summary.shape)


def per_device(
    mamba_x, gate_z, b_in, c_in, dt_raw, a_log, skip_d, norm_gain, value_weight, queries, keys
):
    tokens_here = mamba_x.shape[0]
    group_count = b_in.shape[1] // STATE
    head_count = dt_raw.shape[0]
    per_group = head_count // group_count
    inputs = mamba_x.astype(jnp.float32).reshape(tokens_here, group_count, per_group, MHEAD_DIM)
    b_group = b_in.astype(jnp.float32).reshape(tokens_here, group_count, STATE)
    c_group = c_in.astype(jnp.float32).reshape(tokens_here, group_count, STATE)
    time_step = jax.nn.softplus(dt_raw).reshape(group_count, per_group, tokens_here)
    decay_rate = jnp.exp(a_log).reshape(group_count, per_group)
    log_decay, local_out, summary, totals = block_scan(
        inputs, b_group, c_group, time_step, decay_rate
    )
    state_in = carried_state(totals, summary)
    skip_heads = skip_d.reshape(group_count, per_group)[None, :, :, None]
    ssm_out = local_out + carried_out(c_group, state_in, log_decay) + skip_heads * inputs
    mamba_out = gated_norm(ssm_out.reshape(tokens_here, -1), gate_z, norm_gain, group_count)
    kv_here = keys.shape[1] // HEAD_DIM
    per_kv = QHEADS // KVHEADS
    tp_count = lax.axis_size("tp")
    product = jnp.dot(mamba_out, value_weight, preferred_element_type=jnp.float32)
    partials = jnp.transpose(
        product.reshape(tokens_here, tp_count, kv_here * HEAD_DIM), (1, 0, 2)
    )
    exchanged = lax.all_to_all(partials, "tp", 0, 0, tiled=True)
    values = jnp.sum(exchanged, axis=0).astype(jnp.bfloat16)
    values = jnp.transpose(values.reshape(tokens_here, kv_here, HEAD_DIM), (1, 0, 2))
    key_heads = jnp.transpose(keys.reshape(tokens_here, kv_here, HEAD_DIM), (1, 0, 2))
    pair = jnp.stack([key_heads, values])
    for axis in SEQ_AXES[::-1]:
        pair = gather_by_exchange(pair, axis)
    all_pairs = jnp.transpose(pair, (3, 4, 2, 1, 0, 5, 6)).reshape(2, kv_here, -1, HEAD_DIM)
    key_portion = all_pairs[0]
    value_portion = all_pairs[1]
    my_index = lax.axis_index(SEQ_AXES[::-1])
    query_sets = [
        (
            query_layout(queries, kv_here, per_kv),
            row_positions(my_index * tokens_here, tokens_here, per_kv),
        )
    ]
    initial = tuple(
        (
            (
                jnp.full((kv_here, query_set[0].shape[1]), -jnp.inf, jnp.float32),
                jnp.zeros((kv_here, query_set[0].shape[1]), jnp.float32),
                jnp.zeros((kv_here, query_set[0].shape[1], HEAD_DIM), jnp.float32),
            )
            for query_set in query_sets
        )
    )
    length = key_portion.shape[1]
    block_len = length
    for multiple in (1, 2, 4):
        block_len = multiple * tokens_here

    def one_block(block_index, current):
        offset = block_index * block_len
        key_slab = lax.dynamic_slice_in_dim(key_portion, offset, block_len, 1)
        value_slab = lax.dynamic_slice_in_dim(value_portion, offset, block_len, 1)
        return tuple(
            (
                attend(current[set_index], query_sets[set_index], key_slab, value_slab, offset)
                for set_index in range(len(query_sets))
            )
        )

    finished = lax.fori_loop(0, length // block_len, one_block, initial)
    outputs = [set_output(finished_set, kv_here, per_kv) for finished_set in finished]
    attention = outputs[0]
    return (mamba_out, attention)


def solution(mesh):
    seq_count = mesh.shape["seq"]
    split = Mesh(
        mesh.devices.reshape(seq_count // 16, 4, 4, mesh.shape["tp"]),
        SEQ_AXES[::-1] + ("tp",),
    )
    rows = SEQ_AXES[::-1]
    placed = (
        P(rows, "tp"),
        P(rows, "tp"),
        P(rows, "tp"),
        P(rows, "tp"),
        P("tp", rows),
        P("tp"),
        P("tp"),
        P("tp"),
        P("tp", None),
        P(rows, "tp"),
        P(rows, "tp"),
    )
    return jax.shard_map(
        per_device,
        mesh=split,
        in_specs=placed,
        out_specs=(P(rows, "tp"), P(rows, "tp")),
        check_vma=False,
    )
```

```python
import math

import jax
import jax.numpy as jnp
from jax import lax
from jax.sharding import Mesh, PartitionSpec as P

MHEAD_DIM = 64
STATE = 128
QHEADS = 32
KVHEADS = 8
HEAD_DIM = 128
SEQ_AXES = (("zl", "sx"), "zh")
ROWS = ("zh", "zl", "sx")


highest = lax.Precision.HIGHEST
norm_eps = 1e-05


def block_scan(inputs, b_group, c_group, time_step, decay_rate):
    token_count = inputs.shape[0]
    log_decay = jnp.cumsum(-time_step * decay_rate[..., None], axis=2)
    log_gaps = log_decay[..., :, None] - log_decay[..., None, :]
    causal = jnp.arange(token_count)[:, None] >= jnp.arange(token_count)[None, :]
    decay_mat = jnp.exp(jnp.where(causal, log_gaps, -jnp.inf))
    cross_terms = jnp.einsum("tgn,sgn->gts", c_group, b_group, precision=highest)
    mixing = cross_terms[:, None] * decay_mat * time_step[:, :, None, :]
    local_out = jnp.einsum("gkts,sgkp->tgkp", mixing, inputs, precision=highest)
    tail_weight = jnp.exp(log_decay[..., -1:] - log_decay) * time_step
    summary = jnp.einsum("gks,sgkp,sgn->gkpn", tail_weight, inputs, b_group, precision=highest)
    return (log_decay, local_out, summary, jnp.exp(log_decay[..., -1]))


def carried_out(c_group, state_in, log_decay):
    carried_term = jnp.einsum("tgn,gkpn->tgkp", c_group, state_in, precision=highest)
    return carried_term * jnp.transpose(jnp.exp(log_decay), (2, 0, 1))[..., None]


def gated_norm(ssm_out, gate_z, norm_gain, group_count):
    token_count = ssm_out.shape[0]
    gated = ssm_out * jax.nn.silu(gate_z.astype(jnp.float32))
    grouped = gated.reshape(token_count, group_count, -1)
    inverse = lax.rsqrt(jnp.mean(grouped * grouped, axis=2, keepdims=True) + norm_eps)
    return ((grouped * inverse).reshape(token_count, -1) * norm_gain).astype(jnp.bfloat16)


def query_layout(payload, kv_here, per_kv):
    count_rows = payload.shape[0]
    shaped = payload.reshape(count_rows, kv_here, per_kv, HEAD_DIM)
    return jnp.transpose(shaped, (1, 2, 0, 3)).reshape(kv_here, per_kv * count_rows, HEAD_DIM)


def row_positions(first_pos, count_rows, per_kv):
    return jnp.tile(first_pos + jnp.arange(count_rows, dtype=jnp.int32), per_kv)


def set_output(finished_set, kv_here, per_kv):
    running_max, running_sum, running_out = finished_set
    count_rows = running_sum.shape[1] // per_kv
    result = (running_out / running_sum[..., None]).astype(jnp.bfloat16)
    result = result.reshape(kv_here, per_kv, count_rows, HEAD_DIM)
    return jnp.transpose(result, (2, 0, 1, 3)).reshape(count_rows, kv_here * per_kv * HEAD_DIM)


def attend(running, query_set, key_slab, value_slab, key_first):
    query_block, query_pos = query_set
    score_scale = 1.0 / math.sqrt(HEAD_DIM)
    key_pos = key_first + jnp.arange(key_slab.shape[1], dtype=jnp.int32)

    def update(current):
        running_max, running_sum, running_out = current
        scores = (
            jnp.einsum("hrd,hcd->hrc", query_block, key_slab, preferred_element_type=jnp.float32)
            * score_scale
        )
        allowed = key_pos[None, :] <= query_pos[:, None]
        scores = jnp.where(allowed[None], scores, -jnp.inf)
        new_max = jnp.maximum(running_max, jnp.max(scores, axis=2))
        weights = jnp.exp(scores - new_max[..., None])
        shrink = jnp.exp(running_max - new_max)
        new_sum = running_sum * shrink + jnp.sum(weights, axis=2)
        new_out = running_out * shrink[..., None] + jnp.einsum(
            "hrc,hcd->hrd",
            weights.astype(jnp.bfloat16),
            value_slab,
            preferred_element_type=jnp.float32,
        )
        return (new_max, new_sum, new_out)

    def unchanged(current):
        return current

    return lax.cond(key_first <= jnp.max(query_pos), update, unchanged, running)


def gather_by_exchange(block, axis):
    count = lax.axis_size(axis)
    repeated = jnp.broadcast_to(block[None], (count,) + block.shape)
    return lax.all_to_all(repeated, axis, 0, 0, tiled=True)


def masked_weights(decays, upto):
    count = decays.shape[0]
    earlier = jnp.arange(count)[:, None]
    later = jnp.arange(count)[None, :]
    between = (later > earlier) & (later < upto)
    spans = jnp.prod(jnp.where(between[:, :, None], decays[None, :, :], 1.0), axis=1)
    return jnp.where((jnp.arange(count) < upto)[:, None], spans, 0.0)


def pack_decay(state, decay):
    lanes = 128
    return jnp.concatenate(
        [state, jnp.broadcast_to(decay[..., None], decay.shape + (lanes,))], axis=-1
    )


def entering_top(axis, decay, state):
    width = state.shape[1]
    gathered = gather_by_exchange(pack_decay(state, decay), axis)
    weights = masked_weights(gathered[:, :, width], lax.axis_index(axis))
    return jnp.sum(weights[:, :, None] * gathered[:, :, :width], axis=0)


def entering_state(axes, decay, state):
    if len(axes) == 1:
        return entering_top(axes[0], decay, state)
    axis = axes[0]
    count = lax.axis_size(axis)
    head_total, width = state.shape
    chunk = width // count
    pieces = jnp.transpose(state.reshape(head_total, count, chunk), (1, 0, 2))
    packed = pack_decay(pieces, jnp.broadcast_to(decay, (count, head_total)))
    received = lax.all_to_all(packed, axis, 0, 0, tiled=True)
    decays = received[:, :, chunk]
    states = received[:, :, :chunk]
    member = jnp.arange(count)
    prefixes = [
        jnp.sum(masked_weights(decays, upto)[:, :, None] * states, axis=0)
        for upto in range(count + 1)
    ]
    decay_before = [
        jnp.prod(jnp.where((member < upto)[:, None], decays, 1.0), axis=0)
        for upto in range(count + 1)
    ]
    group_in = entering_state(axes[1:], decay_before[count], prefixes[count])
    outgoing = jnp.stack(
        [decay_before[upto][:, None] * group_in + prefixes[upto] for upto in range(count)]
    )
    returned = lax.all_to_all(outgoing, axis, 0, 0, tiled=True)
    return jnp.transpose(returned, (1, 0, 2)).reshape(head_total, width)


def carried_state(totals, summary):
    head_total = totals.size
    state_in = entering_state(SEQ_AXES, totals.reshape(head_total), summary.reshape(head_total, -1))
    return state_in.reshape(summary.shape)


def per_device(
    mamba_x, gate_z, b_in, c_in, dt_raw, a_log, skip_d, norm_gain, value_weight, queries, keys
):
    tokens_here = mamba_x.shape[0]
    group_count = b_in.shape[1] // STATE
    head_count = dt_raw.shape[0]
    per_group = head_count // group_count
    inputs = mamba_x.astype(jnp.float32).reshape(tokens_here, group_count, per_group, MHEAD_DIM)
    b_group = b_in.astype(jnp.float32).reshape(tokens_here, group_count, STATE)
    c_group = c_in.astype(jnp.float32).reshape(tokens_here, group_count, STATE)
    time_step = jax.nn.softplus(dt_raw).reshape(group_count, per_group, tokens_here)
    decay_rate = jnp.exp(a_log).reshape(group_count, per_group)
    log_decay, local_out, summary, totals = block_scan(
        inputs, b_group, c_group, time_step, decay_rate
    )
    state_in = carried_state(totals, summary)
    skip_heads = skip_d.reshape(group_count, per_group)[None, :, :, None]
    ssm_out = local_out + carried_out(c_group, state_in, log_decay) + skip_heads * inputs
    mamba_out = gated_norm(ssm_out.reshape(tokens_here, -1), gate_z, norm_gain, group_count)
    kv_here = keys.shape[1] // HEAD_DIM
    per_kv = QHEADS // KVHEADS
    tp_count = lax.axis_size("tp")
    product = jnp.dot(mamba_out, value_weight, preferred_element_type=jnp.float32)
    partials = jnp.transpose(
        product.reshape(tokens_here, tp_count, kv_here * HEAD_DIM), (1, 0, 2)
    )
    exchanged = lax.all_to_all(partials, "tp", 0, 0, tiled=True)
    values = jnp.sum(exchanged, axis=0).astype(jnp.bfloat16)
    values = jnp.transpose(values.reshape(tokens_here, kv_here, HEAD_DIM), (1, 0, 2))
    key_heads = jnp.transpose(keys.reshape(tokens_here, kv_here, HEAD_DIM), (1, 0, 2))
    pair = jnp.stack([key_heads, values])
    pair = gather_by_exchange(gather_by_exchange(pair, "zh"), ("zl", "sx"))
    all_pairs = jnp.transpose(pair, (2, 3, 1, 0, 4, 5)).reshape(2, kv_here, -1, HEAD_DIM)
    key_portion = all_pairs[0]
    value_portion = all_pairs[1]
    my_index = lax.axis_index(ROWS)
    query_sets = [
        (
            query_layout(queries, kv_here, per_kv),
            row_positions(my_index * tokens_here, tokens_here, per_kv),
        )
    ]
    initial = tuple(
        (
            (
                jnp.full((kv_here, query_set[0].shape[1]), -jnp.inf, jnp.float32),
                jnp.zeros((kv_here, query_set[0].shape[1]), jnp.float32),
                jnp.zeros((kv_here, query_set[0].shape[1], HEAD_DIM), jnp.float32),
            )
            for query_set in query_sets
        )
    )
    length = key_portion.shape[1]
    block_len = length
    for multiple in (1, 2, 4):
        block_len = multiple * tokens_here

    def one_block(block_index, current):
        offset = block_index * block_len
        key_slab = lax.dynamic_slice_in_dim(key_portion, offset, block_len, 1)
        value_slab = lax.dynamic_slice_in_dim(value_portion, offset, block_len, 1)
        return tuple(
            (
                attend(current[set_index], query_sets[set_index], key_slab, value_slab, offset)
                for set_index in range(len(query_sets))
            )
        )

    finished = lax.fori_loop(0, length // block_len, one_block, initial)
    outputs = [set_output(finished_set, kv_here, per_kv) for finished_set in finished]
    attention = outputs[0]
    return (mamba_out, attention)


def solution(mesh):
    seq_count = mesh.shape["seq"]
    split = Mesh(
        mesh.devices.reshape(seq_count // 16, 4, 4, mesh.shape["tp"]),
        ROWS + ("tp",),
    )
    rows = ROWS
    placed = (
        P(rows, "tp"),
        P(rows, "tp"),
        P(rows, "tp"),
        P(rows, "tp"),
        P("tp", rows),
        P("tp"),
        P("tp"),
        P("tp"),
        P("tp", None),
        P(rows, "tp"),
        P(rows, "tp"),
    )
    return jax.shard_map(
        per_device,
        mesh=split,
        in_specs=placed,
        out_specs=(P(rows, "tp"), P(rows, "tp")),
        check_vma=False,
    )
```

```python
import math

import jax
import jax.numpy as jnp
from jax import lax
from jax.sharding import Mesh, PartitionSpec as P

MHEAD_DIM = 64
STATE = 128
QHEADS = 32
KVHEADS = 8
HEAD_DIM = 128
SEQ_AXES = ("sx", "zl", "zh")


highest = lax.Precision.HIGHEST
norm_eps = 1e-05


def block_scan(inputs, b_group, c_group, time_step, decay_rate):
    token_count = inputs.shape[0]
    log_decay = jnp.cumsum(-time_step * decay_rate[..., None], axis=2)
    log_gaps = log_decay[..., :, None] - log_decay[..., None, :]
    causal = jnp.arange(token_count)[:, None] >= jnp.arange(token_count)[None, :]
    decay_mat = jnp.exp(jnp.where(causal, log_gaps, -jnp.inf))
    cross_terms = jnp.einsum("tgn,sgn->gts", c_group, b_group, precision=highest)
    mixing = cross_terms[:, None] * decay_mat * time_step[:, :, None, :]
    local_out = jnp.einsum("gkts,sgkp->tgkp", mixing, inputs, precision=highest)
    tail_weight = jnp.exp(log_decay[..., -1:] - log_decay) * time_step
    summary = jnp.einsum("gks,sgkp,sgn->gkpn", tail_weight, inputs, b_group, precision=highest)
    return (log_decay, local_out, summary, jnp.exp(log_decay[..., -1]))


def carried_out(c_group, state_in, log_decay):
    carried_term = jnp.einsum("tgn,gkpn->tgkp", c_group, state_in, precision=highest)
    return carried_term * jnp.transpose(jnp.exp(log_decay), (2, 0, 1))[..., None]


def gated_norm(ssm_out, gate_z, norm_gain, group_count):
    token_count = ssm_out.shape[0]
    gated = ssm_out * jax.nn.silu(gate_z.astype(jnp.float32))
    grouped = gated.reshape(token_count, group_count, -1)
    inverse = lax.rsqrt(jnp.mean(grouped * grouped, axis=2, keepdims=True) + norm_eps)
    return ((grouped * inverse).reshape(token_count, -1) * norm_gain).astype(jnp.bfloat16)


def query_layout(payload, kv_here, per_kv):
    count_rows = payload.shape[0]
    shaped = payload.reshape(count_rows, kv_here, per_kv, HEAD_DIM)
    return jnp.transpose(shaped, (1, 2, 0, 3)).reshape(kv_here, per_kv * count_rows, HEAD_DIM)


def row_positions(first_pos, count_rows, per_kv):
    return jnp.tile(first_pos + jnp.arange(count_rows, dtype=jnp.int32), per_kv)


def set_output(finished_set, kv_here, per_kv):
    running_max, running_sum, running_out = finished_set
    count_rows = running_sum.shape[1] // per_kv
    result = (running_out / running_sum[..., None]).astype(jnp.bfloat16)
    result = result.reshape(kv_here, per_kv, count_rows, HEAD_DIM)
    return jnp.transpose(result, (2, 0, 1, 3)).reshape(count_rows, kv_here * per_kv * HEAD_DIM)


def attend(running, query_set, key_slab, value_slab, key_first):
    query_block, query_pos = query_set
    score_scale = 1.0 / math.sqrt(HEAD_DIM)
    key_pos = key_first + jnp.arange(key_slab.shape[1], dtype=jnp.int32)

    def update(current):
        running_max, running_sum, running_out = current
        scores = (
            jnp.einsum("hrd,hcd->hrc", query_block, key_slab, preferred_element_type=jnp.float32)
            * score_scale
        )
        allowed = key_pos[None, :] <= query_pos[:, None]
        scores = jnp.where(allowed[None], scores, -jnp.inf)
        new_max = jnp.maximum(running_max, jnp.max(scores, axis=2))
        weights = jnp.exp(scores - new_max[..., None])
        shrink = jnp.exp(running_max - new_max)
        new_sum = running_sum * shrink + jnp.sum(weights, axis=2)
        new_out = running_out * shrink[..., None] + jnp.einsum(
            "hrc,hcd->hrd",
            weights.astype(jnp.bfloat16),
            value_slab,
            preferred_element_type=jnp.float32,
        )
        return (new_max, new_sum, new_out)

    def unchanged(current):
        return current

    return lax.cond(key_first <= jnp.max(query_pos), update, unchanged, running)


def gather_by_exchange(block, axis):
    count = lax.axis_size(axis)
    repeated = jnp.broadcast_to(block[None], (count,) + block.shape)
    return lax.all_to_all(repeated, axis, 0, 0, tiled=True)


def gather_shifted(block, axis, wrap):
    count = lax.axis_size(axis)
    here = lax.axis_index(axis)
    shifted = [block]
    for shift in range(1, count):
        last = count if wrap else count - shift
        pairs = [(source, (source + shift) % count) for source in range(last)]
        shifted.append(lax.ppermute(block, axis, pairs))
    stacked = jnp.stack(shifted)
    return stacked[(here - jnp.arange(count)) % count]


def masked_weights(decays, upto):
    count = decays.shape[0]
    earlier = jnp.arange(count)[:, None]
    later = jnp.arange(count)[None, :]
    between = (later > earlier) & (later < upto)
    spans = jnp.prod(jnp.where(between[:, :, None], decays[None, :, :], 1.0), axis=1)
    return jnp.where((jnp.arange(count) < upto)[:, None], spans, 0.0)


def pack_decay(state, decay):
    lanes = 128
    return jnp.concatenate(
        [state, jnp.broadcast_to(decay[..., None], decay.shape + (lanes,))], axis=-1
    )


def entering_top(axis, decay, state):
    width = state.shape[1]
    gathered = gather_shifted(pack_decay(state, decay), axis, False)
    weights = masked_weights(gathered[:, :, width], lax.axis_index(axis))
    return jnp.sum(weights[:, :, None] * gathered[:, :, :width], axis=0)


def entering_state(axes, decay, state):
    if len(axes) == 1:
        return entering_top(axes[0], decay, state)
    axis = axes[0]
    count = lax.axis_size(axis)
    head_total, width = state.shape
    chunk = width // count
    pieces = jnp.transpose(state.reshape(head_total, count, chunk), (1, 0, 2))
    packed = pack_decay(pieces, jnp.broadcast_to(decay, (count, head_total)))
    received = lax.all_to_all(packed, axis, 0, 0, tiled=True)
    decays = received[:, :, chunk]
    states = received[:, :, :chunk]
    member = jnp.arange(count)
    prefixes = [
        jnp.sum(masked_weights(decays, upto)[:, :, None] * states, axis=0)
        for upto in range(count + 1)
    ]
    decay_before = [
        jnp.prod(jnp.where((member < upto)[:, None], decays, 1.0), axis=0)
        for upto in range(count + 1)
    ]
    group_in = entering_state(axes[1:], decay_before[count], prefixes[count])
    outgoing = jnp.stack(
        [decay_before[upto][:, None] * group_in + prefixes[upto] for upto in range(count)]
    )
    returned = lax.all_to_all(outgoing, axis, 0, 0, tiled=True)
    return jnp.transpose(returned, (1, 0, 2)).reshape(head_total, width)


def carried_state(totals, summary):
    head_total = totals.size
    state_in = entering_state(SEQ_AXES, totals.reshape(head_total), summary.reshape(head_total, -1))
    return state_in.reshape(summary.shape)


def per_device(
    mamba_x, gate_z, b_in, c_in, dt_raw, a_log, skip_d, norm_gain, value_weight, queries, keys
):
    tokens_here = mamba_x.shape[0]
    group_count = b_in.shape[1] // STATE
    head_count = dt_raw.shape[0]
    per_group = head_count // group_count
    inputs = mamba_x.astype(jnp.float32).reshape(tokens_here, group_count, per_group, MHEAD_DIM)
    b_group = b_in.astype(jnp.float32).reshape(tokens_here, group_count, STATE)
    c_group = c_in.astype(jnp.float32).reshape(tokens_here, group_count, STATE)
    time_step = jax.nn.softplus(dt_raw).reshape(group_count, per_group, tokens_here)
    decay_rate = jnp.exp(a_log).reshape(group_count, per_group)
    log_decay, local_out, summary, totals = block_scan(
        inputs, b_group, c_group, time_step, decay_rate
    )
    state_in = carried_state(totals, summary)
    skip_heads = skip_d.reshape(group_count, per_group)[None, :, :, None]
    ssm_out = local_out + carried_out(c_group, state_in, log_decay) + skip_heads * inputs
    mamba_out = gated_norm(ssm_out.reshape(tokens_here, -1), gate_z, norm_gain, group_count)
    kv_here = keys.shape[1] // HEAD_DIM
    per_kv = QHEADS // KVHEADS
    tp_count = lax.axis_size("tp")
    product = jnp.dot(mamba_out, value_weight, preferred_element_type=jnp.float32)
    partials = jnp.transpose(
        product.reshape(tokens_here, tp_count, kv_here * HEAD_DIM), (1, 0, 2)
    )
    exchanged = lax.all_to_all(partials, "tp", 0, 0, tiled=True)
    values = jnp.sum(exchanged, axis=0).astype(jnp.bfloat16)
    values = jnp.transpose(values.reshape(tokens_here, kv_here, HEAD_DIM), (1, 0, 2))
    key_heads = jnp.transpose(keys.reshape(tokens_here, kv_here, HEAD_DIM), (1, 0, 2))
    pair = jnp.stack([key_heads, values])
    pair = gather_shifted(pair, "zh", False)
    pair = gather_shifted(pair, "zl", True)
    pair = gather_by_exchange(pair, "sx")
    all_pairs = jnp.transpose(pair, (3, 4, 2, 1, 0, 5, 6)).reshape(2, kv_here, -1, HEAD_DIM)
    key_portion = all_pairs[0]
    value_portion = all_pairs[1]
    my_index = lax.axis_index(SEQ_AXES[::-1])
    query_sets = [
        (
            query_layout(queries, kv_here, per_kv),
            row_positions(my_index * tokens_here, tokens_here, per_kv),
        )
    ]
    initial = tuple(
        (
            (
                jnp.full((kv_here, query_set[0].shape[1]), -jnp.inf, jnp.float32),
                jnp.zeros((kv_here, query_set[0].shape[1]), jnp.float32),
                jnp.zeros((kv_here, query_set[0].shape[1], HEAD_DIM), jnp.float32),
            )
            for query_set in query_sets
        )
    )
    length = key_portion.shape[1]
    block_len = length
    for multiple in (1, 2, 4):
        block_len = multiple * tokens_here

    def one_block(block_index, current):
        offset = block_index * block_len
        key_slab = lax.dynamic_slice_in_dim(key_portion, offset, block_len, 1)
        value_slab = lax.dynamic_slice_in_dim(value_portion, offset, block_len, 1)
        return tuple(
            (
                attend(current[set_index], query_sets[set_index], key_slab, value_slab, offset)
                for set_index in range(len(query_sets))
            )
        )

    finished = lax.fori_loop(0, length // block_len, one_block, initial)
    outputs = [set_output(finished_set, kv_here, per_kv) for finished_set in finished]
    attention = outputs[0]
    return (mamba_out, attention)


def solution(mesh):
    seq_count = mesh.shape["seq"]
    split = Mesh(
        mesh.devices.reshape(seq_count // 16, 4, 4, mesh.shape["tp"]),
        SEQ_AXES[::-1] + ("tp",),
    )
    rows = SEQ_AXES[::-1]
    placed = (
        P(rows, "tp"),
        P(rows, "tp"),
        P(rows, "tp"),
        P(rows, "tp"),
        P("tp", rows),
        P("tp"),
        P("tp"),
        P("tp"),
        P("tp", None),
        P(rows, "tp"),
        P(rows, "tp"),
    )
    return jax.shard_map(
        per_device,
        mesh=split,
        in_specs=placed,
        out_specs=(P(rows, "tp"), P(rows, "tp")),
        check_vma=False,
    )
```

```python
import math

import jax
import jax.numpy as jnp
from jax import lax
from jax.sharding import Mesh, PartitionSpec as P

MHEAD_DIM = 64
STATE = 128
QHEADS = 32
KVHEADS = 8
HEAD_DIM = 128
SEQ_AXES = ("sx", "zl", "zh")


highest = lax.Precision.HIGHEST
norm_eps = 1e-05


def block_scan(inputs, b_group, c_group, time_step, decay_rate):
    token_count = inputs.shape[0]
    log_decay = jnp.cumsum(-time_step * decay_rate[..., None], axis=2)
    log_gaps = log_decay[..., :, None] - log_decay[..., None, :]
    causal = jnp.arange(token_count)[:, None] >= jnp.arange(token_count)[None, :]
    decay_mat = jnp.exp(jnp.where(causal, log_gaps, -jnp.inf))
    cross_terms = jnp.einsum("tgn,sgn->gts", c_group, b_group, precision=highest)
    mixing = cross_terms[:, None] * decay_mat * time_step[:, :, None, :]
    local_out = jnp.einsum("gkts,sgkp->tgkp", mixing, inputs, precision=highest)
    tail_weight = jnp.exp(log_decay[..., -1:] - log_decay) * time_step
    summary = jnp.einsum("gks,sgkp,sgn->gkpn", tail_weight, inputs, b_group, precision=highest)
    return (log_decay, local_out, summary, jnp.exp(log_decay[..., -1]))


def carried_out(c_group, state_in, log_decay):
    carried_term = jnp.einsum("tgn,gkpn->tgkp", c_group, state_in, precision=highest)
    return carried_term * jnp.transpose(jnp.exp(log_decay), (2, 0, 1))[..., None]


def gated_norm(ssm_out, gate_z, norm_gain, group_count):
    token_count = ssm_out.shape[0]
    gated = ssm_out * jax.nn.silu(gate_z.astype(jnp.float32))
    grouped = gated.reshape(token_count, group_count, -1)
    inverse = lax.rsqrt(jnp.mean(grouped * grouped, axis=2, keepdims=True) + norm_eps)
    return ((grouped * inverse).reshape(token_count, -1) * norm_gain).astype(jnp.bfloat16)


def query_layout(payload, kv_here, per_kv):
    count_rows = payload.shape[0]
    shaped = payload.reshape(count_rows, kv_here, per_kv, HEAD_DIM)
    return jnp.transpose(shaped, (1, 2, 0, 3)).reshape(kv_here, per_kv * count_rows, HEAD_DIM)


def row_positions(first_pos, count_rows, per_kv):
    return jnp.tile(first_pos + jnp.arange(count_rows, dtype=jnp.int32), per_kv)


def set_output(finished_set, kv_here, per_kv):
    running_max, running_sum, running_out = finished_set
    count_rows = running_sum.shape[1] // per_kv
    result = (running_out / running_sum[..., None]).astype(jnp.bfloat16)
    result = result.reshape(kv_here, per_kv, count_rows, HEAD_DIM)
    return jnp.transpose(result, (2, 0, 1, 3)).reshape(count_rows, kv_here * per_kv * HEAD_DIM)


def gather_by_exchange(block, axis):
    count = lax.axis_size(axis)
    repeated = jnp.broadcast_to(block[None], (count,) + block.shape)
    return lax.all_to_all(repeated, axis, 0, 0, tiled=True)


def masked_weights(decays, upto):
    count = decays.shape[0]
    earlier = jnp.arange(count)[:, None]
    later = jnp.arange(count)[None, :]
    between = (later > earlier) & (later < upto)
    spans = jnp.prod(jnp.where(between[:, :, None], decays[None, :, :], 1.0), axis=1)
    return jnp.where((jnp.arange(count) < upto)[:, None], spans, 0.0)


def pack_decay(state, decay):
    lanes = 128
    return jnp.concatenate(
        [state, jnp.broadcast_to(decay[..., None], decay.shape + (lanes,))], axis=-1
    )


def entering_top(axis, decay, state):
    width = state.shape[1]
    gathered = gather_by_exchange(pack_decay(state, decay), axis)
    weights = masked_weights(gathered[:, :, width], lax.axis_index(axis))
    return jnp.sum(weights[:, :, None] * gathered[:, :, :width], axis=0)


def entering_state(axes, decay, state):
    if len(axes) == 1:
        return entering_top(axes[0], decay, state)
    axis = axes[0]
    count = lax.axis_size(axis)
    head_total, width = state.shape
    chunk = width // count
    pieces = jnp.transpose(state.reshape(head_total, count, chunk), (1, 0, 2))
    packed = pack_decay(pieces, jnp.broadcast_to(decay, (count, head_total)))
    received = lax.all_to_all(packed, axis, 0, 0, tiled=True)
    decays = received[:, :, chunk]
    states = received[:, :, :chunk]
    member = jnp.arange(count)
    prefixes = [
        jnp.sum(masked_weights(decays, upto)[:, :, None] * states, axis=0)
        for upto in range(count + 1)
    ]
    decay_before = [
        jnp.prod(jnp.where((member < upto)[:, None], decays, 1.0), axis=0)
        for upto in range(count + 1)
    ]
    group_in = entering_state(axes[1:], decay_before[count], prefixes[count])
    outgoing = jnp.stack(
        [decay_before[upto][:, None] * group_in + prefixes[upto] for upto in range(count)]
    )
    returned = lax.all_to_all(outgoing, axis, 0, 0, tiled=True)
    return jnp.transpose(returned, (1, 0, 2)).reshape(head_total, width)


def carried_state(totals, summary):
    head_total = totals.size
    state_in = entering_state(SEQ_AXES, totals.reshape(head_total), summary.reshape(head_total, -1))
    return state_in.reshape(summary.shape)


def per_device(
    mamba_x, gate_z, b_in, c_in, dt_raw, a_log, skip_d, norm_gain, value_weight, queries, keys
):
    tokens_here = mamba_x.shape[0]
    group_count = b_in.shape[1] // STATE
    head_count = dt_raw.shape[0]
    per_group = head_count // group_count
    inputs = mamba_x.astype(jnp.float32).reshape(tokens_here, group_count, per_group, MHEAD_DIM)
    b_group = b_in.astype(jnp.float32).reshape(tokens_here, group_count, STATE)
    c_group = c_in.astype(jnp.float32).reshape(tokens_here, group_count, STATE)
    time_step = jax.nn.softplus(dt_raw).reshape(group_count, per_group, tokens_here)
    decay_rate = jnp.exp(a_log).reshape(group_count, per_group)
    log_decay, local_out, summary, totals = block_scan(
        inputs, b_group, c_group, time_step, decay_rate
    )
    state_in = carried_state(totals, summary)
    skip_heads = skip_d.reshape(group_count, per_group)[None, :, :, None]
    ssm_out = local_out + carried_out(c_group, state_in, log_decay) + skip_heads * inputs
    mamba_out = gated_norm(ssm_out.reshape(tokens_here, -1), gate_z, norm_gain, group_count)
    kv_here = keys.shape[1] // HEAD_DIM
    per_kv = QHEADS // KVHEADS
    tp_count = lax.axis_size("tp")
    product = jnp.dot(mamba_out, value_weight, preferred_element_type=jnp.float32)
    partials = jnp.transpose(
        product.reshape(tokens_here, tp_count, kv_here * HEAD_DIM), (1, 0, 2)
    )
    exchanged = lax.all_to_all(partials, "tp", 0, 0, tiled=True)
    values = jnp.sum(exchanged, axis=0).astype(jnp.bfloat16)
    values = jnp.transpose(values.reshape(tokens_here, kv_here, HEAD_DIM), (1, 0, 2))
    key_heads = jnp.transpose(keys.reshape(tokens_here, kv_here, HEAD_DIM), (1, 0, 2))
    pair = jnp.stack([key_heads, values])
    for axis in SEQ_AXES[::-1]:
        pair = gather_by_exchange(pair, axis)
    all_pairs = jnp.transpose(pair, (3, 4, 2, 1, 0, 5, 6)).reshape(2, kv_here, -1, HEAD_DIM)
    key_portion = all_pairs[0]
    value_portion = all_pairs[1]
    my_index = lax.axis_index(SEQ_AXES[::-1])
    query_block = query_layout(queries, kv_here, per_kv)
    query_pos = row_positions(my_index * tokens_here, tokens_here, per_kv)
    key_pos = jnp.arange(key_portion.shape[1], dtype=jnp.int32)
    scores = jnp.einsum(
        "hrd,hcd->hrc", query_block, key_portion, preferred_element_type=jnp.float32
    ) * (1.0 / math.sqrt(HEAD_DIM))
    allowed = key_pos[None, :] <= query_pos[:, None]
    scores = jnp.where(allowed[None], scores, -jnp.inf)
    row_max = jnp.max(scores, axis=2, keepdims=True)
    weights = jnp.exp(scores - row_max)
    total = jnp.sum(weights, axis=2)
    weighted = jnp.einsum(
        "hrc,hcd->hrd", weights.astype(jnp.bfloat16), value_portion, preferred_element_type=jnp.float32
    )
    attention = set_output((row_max, total, weighted), kv_here, per_kv)
    return (mamba_out, attention)


def solution(mesh):
    seq_count = mesh.shape["seq"]
    split = Mesh(
        mesh.devices.reshape(seq_count // 16, 4, 4, mesh.shape["tp"]),
        SEQ_AXES[::-1] + ("tp",),
    )
    rows = SEQ_AXES[::-1]
    placed = (
        P(rows, "tp"),
        P(rows, "tp"),
        P(rows, "tp"),
        P(rows, "tp"),
        P("tp", rows),
        P("tp"),
        P("tp"),
        P("tp"),
        P("tp", None),
        P(rows, "tp"),
        P(rows, "tp"),
    )
    return jax.shard_map(
        per_device,
        mesh=split,
        in_specs=placed,
        out_specs=(P(rows, "tp"), P(rows, "tp")),
        check_vma=False,
    )
```

```python
import math

import jax
import jax.numpy as jnp
from jax import lax
from jax.sharding import Mesh, PartitionSpec as P

MHEAD_DIM = 64
STATE = 128
QHEADS = 32
KVHEADS = 8
HEAD_DIM = 128
SEQ_AXES = ("sx", "zl", "zh")


highest = lax.Precision.HIGHEST
norm_eps = 1e-05


def block_scan(inputs, b_group, c_group, time_step, decay_rate):
    token_count = inputs.shape[0]
    log_decay = jnp.cumsum(-time_step * decay_rate[..., None], axis=2)
    log_gaps = log_decay[..., :, None] - log_decay[..., None, :]
    causal = jnp.arange(token_count)[:, None] >= jnp.arange(token_count)[None, :]
    decay_mat = jnp.exp(jnp.where(causal, log_gaps, -jnp.inf))
    cross_terms = jnp.einsum("tgn,sgn->gts", c_group, b_group, precision=highest)
    mixing = cross_terms[:, None] * decay_mat * time_step[:, :, None, :]
    local_out = jnp.einsum("gkts,sgkp->tgkp", mixing, inputs, precision=highest)
    tail_weight = jnp.exp(log_decay[..., -1:] - log_decay) * time_step
    summary = jnp.einsum("gks,sgkp,sgn->gkpn", tail_weight, inputs, b_group, precision=highest)
    return (log_decay, local_out, summary, jnp.exp(log_decay[..., -1]))


def carried_out(c_group, state_in, log_decay):
    carried_term = jnp.einsum("tgn,gkpn->tgkp", c_group, state_in, precision=highest)
    return carried_term * jnp.transpose(jnp.exp(log_decay), (2, 0, 1))[..., None]


def gated_norm(ssm_out, gate_z, norm_gain, group_count):
    token_count = ssm_out.shape[0]
    gated = ssm_out * jax.nn.silu(gate_z.astype(jnp.float32))
    grouped = gated.reshape(token_count, group_count, -1)
    inverse = lax.rsqrt(jnp.mean(grouped * grouped, axis=2, keepdims=True) + norm_eps)
    return ((grouped * inverse).reshape(token_count, -1) * norm_gain).astype(jnp.bfloat16)


def query_layout(payload, kv_here, per_kv):
    count_rows = payload.shape[0]
    shaped = payload.reshape(count_rows, kv_here, per_kv, HEAD_DIM)
    return jnp.transpose(shaped, (1, 2, 0, 3)).reshape(kv_here, per_kv * count_rows, HEAD_DIM)


def row_positions(first_pos, count_rows, per_kv):
    return jnp.tile(first_pos + jnp.arange(count_rows, dtype=jnp.int32), per_kv)


def set_output(finished_set, kv_here, per_kv):
    running_max, running_sum, running_out = finished_set
    count_rows = running_sum.shape[1] // per_kv
    result = (running_out / running_sum[..., None]).astype(jnp.bfloat16)
    result = result.reshape(kv_here, per_kv, count_rows, HEAD_DIM)
    return jnp.transpose(result, (2, 0, 1, 3)).reshape(count_rows, kv_here * per_kv * HEAD_DIM)


def gather_by_exchange(block, axis):
    count = lax.axis_size(axis)
    repeated = jnp.broadcast_to(block[None], (count,) + block.shape)
    return lax.all_to_all(repeated, axis, 0, 0, tiled=True)


def masked_weights(decays, upto):
    count = decays.shape[0]
    earlier = jnp.arange(count)[:, None]
    later = jnp.arange(count)[None, :]
    between = (later > earlier) & (later < upto)
    spans = jnp.prod(jnp.where(between[:, :, None], decays[None, :, :], 1.0), axis=1)
    return jnp.where((jnp.arange(count) < upto)[:, None], spans, 0.0)


def pack_decay(state, decay):
    extra = jnp.broadcast_to(decay[..., None, None], decay.shape + (8, state.shape[-1]))
    return jnp.concatenate([state, extra], axis=-2)


def entering_top(axis, decay, state):
    rows = state.shape[-2]
    gathered = gather_by_exchange(pack_decay(state, decay), axis)
    weights = masked_weights(gathered[:, :, rows, 0], lax.axis_index(axis))
    return jnp.sum(weights[:, :, None, None] * gathered[:, :, :rows], axis=0)


def entering_state(axes, decay, state):
    if len(axes) == 1:
        return entering_top(axes[0], decay, state)
    axis = axes[0]
    count = lax.axis_size(axis)
    head_total, rows, lanes = state.shape
    part = head_total // count
    packed = pack_decay(state.reshape(count, part, rows, lanes), decay.reshape(count, part))
    received = lax.all_to_all(packed, axis, 0, 0, tiled=True)
    decays = received[:, :, rows, 0]
    states = received[:, :, :rows]
    member = jnp.arange(count)
    prefixes = [
        jnp.sum(masked_weights(decays, upto)[:, :, None, None] * states, axis=0)
        for upto in range(count + 1)
    ]
    decay_before = [
        jnp.prod(jnp.where((member < upto)[:, None], decays, 1.0), axis=0)
        for upto in range(count + 1)
    ]
    group_in = entering_state(axes[1:], decay_before[count], prefixes[count])
    outgoing = jnp.stack(
        [
            decay_before[upto][:, None, None] * group_in + prefixes[upto]
            for upto in range(count)
        ]
    )
    returned = lax.all_to_all(outgoing, axis, 0, 0, tiled=True)
    return returned.reshape(head_total, rows, lanes)


def carried_state(totals, summary):
    head_total = totals.size
    state_in = entering_state(
        SEQ_AXES, totals.reshape(head_total), summary.reshape((head_total,) + summary.shape[-2:])
    )
    return state_in.reshape(summary.shape)


def per_device(
    mamba_x, gate_z, b_in, c_in, dt_raw, a_log, skip_d, norm_gain, value_weight, queries, keys
):
    tokens_here = mamba_x.shape[0]
    group_count = b_in.shape[1] // STATE
    head_count = dt_raw.shape[0]
    per_group = head_count // group_count
    inputs = mamba_x.astype(jnp.float32).reshape(tokens_here, group_count, per_group, MHEAD_DIM)
    b_group = b_in.astype(jnp.float32).reshape(tokens_here, group_count, STATE)
    c_group = c_in.astype(jnp.float32).reshape(tokens_here, group_count, STATE)
    time_step = jax.nn.softplus(dt_raw).reshape(group_count, per_group, tokens_here)
    decay_rate = jnp.exp(a_log).reshape(group_count, per_group)
    log_decay, local_out, summary, totals = block_scan(
        inputs, b_group, c_group, time_step, decay_rate
    )
    state_in = carried_state(totals, summary)
    skip_heads = skip_d.reshape(group_count, per_group)[None, :, :, None]
    ssm_out = local_out + carried_out(c_group, state_in, log_decay) + skip_heads * inputs
    mamba_out = gated_norm(ssm_out.reshape(tokens_here, -1), gate_z, norm_gain, group_count)
    kv_here = keys.shape[1] // HEAD_DIM
    per_kv = QHEADS // KVHEADS
    tp_count = lax.axis_size("tp")
    product = jnp.dot(mamba_out, value_weight, preferred_element_type=jnp.float32)
    partials = jnp.transpose(
        product.reshape(tokens_here, tp_count, kv_here * HEAD_DIM), (1, 0, 2)
    )
    exchanged = lax.all_to_all(partials, "tp", 0, 0, tiled=True)
    values = jnp.sum(exchanged, axis=0).astype(jnp.bfloat16)
    values = jnp.transpose(values.reshape(tokens_here, kv_here, HEAD_DIM), (1, 0, 2))
    key_heads = jnp.transpose(keys.reshape(tokens_here, kv_here, HEAD_DIM), (1, 0, 2))
    pair = jnp.stack([key_heads, values])
    for axis in SEQ_AXES[::-1]:
        pair = gather_by_exchange(pair, axis)
    all_pairs = jnp.transpose(pair, (3, 4, 2, 1, 0, 5, 6)).reshape(2, kv_here, -1, HEAD_DIM)
    key_portion = all_pairs[0]
    value_portion = all_pairs[1]
    my_index = lax.axis_index(SEQ_AXES[::-1])
    query_block = query_layout(queries, kv_here, per_kv)
    query_pos = row_positions(my_index * tokens_here, tokens_here, per_kv)
    key_pos = jnp.arange(key_portion.shape[1], dtype=jnp.int32)
    scores = jnp.einsum(
        "hrd,hcd->hrc", query_block, key_portion, preferred_element_type=jnp.float32
    ) * (1.0 / math.sqrt(HEAD_DIM))
    allowed = key_pos[None, :] <= query_pos[:, None]
    scores = jnp.where(allowed[None], scores, -jnp.inf)
    row_max = jnp.max(scores, axis=2, keepdims=True)
    weights = jnp.exp(scores - row_max)
    total = jnp.sum(weights, axis=2)
    weighted = jnp.einsum(
        "hrc,hcd->hrd", weights.astype(jnp.bfloat16), value_portion, preferred_element_type=jnp.float32
    )
    attention = set_output((row_max, total, weighted), kv_here, per_kv)
    return (mamba_out, attention)


def solution(mesh):
    seq_count = mesh.shape["seq"]
    split = Mesh(
        mesh.devices.reshape(seq_count // 16, 4, 4, mesh.shape["tp"]),
        SEQ_AXES[::-1] + ("tp",),
    )
    rows = SEQ_AXES[::-1]
    placed = (
        P(rows, "tp"),
        P(rows, "tp"),
        P(rows, "tp"),
        P(rows, "tp"),
        P("tp", rows),
        P("tp"),
        P("tp"),
        P("tp"),
        P("tp", None),
        P(rows, "tp"),
        P(rows, "tp"),
    )
    return jax.shard_map(
        per_device,
        mesh=split,
        in_specs=placed,
        out_specs=(P(rows, "tp"), P(rows, "tp")),
        check_vma=False,
    )
```

```python
import math

import jax
import jax.numpy as jnp
from jax import lax
from jax.sharding import Mesh, PartitionSpec as P

MHEAD_DIM = 64
STATE = 128
QHEADS = 32
KVHEADS = 8
HEAD_DIM = 128
SEQ_AXES = ("sx", "zl", "zh")


highest = lax.Precision.HIGHEST
norm_eps = 1e-05


def block_scan(inputs, b_group, c_group, time_step, decay_rate):
    token_count = inputs.shape[0]
    log_decay = jnp.cumsum(-time_step * decay_rate[..., None], axis=2)
    log_gaps = log_decay[..., :, None] - log_decay[..., None, :]
    causal = jnp.arange(token_count)[:, None] >= jnp.arange(token_count)[None, :]
    decay_mat = jnp.exp(jnp.where(causal, log_gaps, -jnp.inf))
    cross_terms = jnp.einsum("tgn,sgn->gts", c_group, b_group, precision=highest)
    mixing = cross_terms[:, None] * decay_mat * time_step[:, :, None, :]
    local_out = jnp.einsum("gkts,sgkp->tgkp", mixing, inputs, precision=highest)
    tail_weight = jnp.exp(log_decay[..., -1:] - log_decay) * time_step
    summary = jnp.einsum("gks,sgkp,sgn->gkpn", tail_weight, inputs, b_group, precision=highest)
    return (log_decay, local_out, summary, jnp.exp(log_decay[..., -1]))


def carried_out(c_group, state_in, log_decay):
    carried_term = jnp.einsum("tgn,gkpn->tgkp", c_group, state_in, precision=highest)
    return carried_term * jnp.transpose(jnp.exp(log_decay), (2, 0, 1))[..., None]


def gated_norm(ssm_out, gate_z, norm_gain, group_count):
    token_count = ssm_out.shape[0]
    gated = ssm_out * jax.nn.silu(gate_z.astype(jnp.float32))
    grouped = gated.reshape(token_count, group_count, -1)
    inverse = lax.rsqrt(jnp.mean(grouped * grouped, axis=2, keepdims=True) + norm_eps)
    return ((grouped * inverse).reshape(token_count, -1) * norm_gain).astype(jnp.bfloat16)


def query_layout(payload, kv_here, per_kv):
    count_rows = payload.shape[0]
    shaped = payload.reshape(count_rows, kv_here, per_kv, HEAD_DIM)
    return jnp.transpose(shaped, (1, 2, 0, 3)).reshape(kv_here, per_kv * count_rows, HEAD_DIM)


def row_positions(first_pos, count_rows, per_kv):
    return jnp.tile(first_pos + jnp.arange(count_rows, dtype=jnp.int32), per_kv)


def set_output(finished_set, kv_here, per_kv):
    running_max, running_sum, running_out = finished_set
    count_rows = running_sum.shape[1] // per_kv
    result = (running_out / running_sum[..., None]).astype(jnp.bfloat16)
    result = result.reshape(kv_here, per_kv, count_rows, HEAD_DIM)
    return jnp.transpose(result, (2, 0, 1, 3)).reshape(count_rows, kv_here * per_kv * HEAD_DIM)


def gather_by_exchange(block, axis):
    count = lax.axis_size(axis)
    repeated = jnp.broadcast_to(block[None], (count,) + block.shape)
    return lax.all_to_all(repeated, axis, 0, 0, tiled=True)


def masked_weights(decays, upto):
    count = decays.shape[0]
    earlier = jnp.arange(count)[:, None]
    later = jnp.arange(count)[None, :]
    between = (later > earlier) & (later < upto)
    spans = jnp.prod(jnp.where(between[:, :, None], decays[None, :, :], 1.0), axis=1)
    return jnp.where((jnp.arange(count) < upto)[:, None], spans, 0.0)


def pack_decay(state, decay):
    extra = jnp.broadcast_to(decay[..., None, None], decay.shape + (8, state.shape[-1]))
    return jnp.concatenate([state, extra], axis=-2)


def entering_top(axis, decay, state):
    rows = state.shape[-2]
    gathered = gather_by_exchange(pack_decay(state, decay), axis)
    weights = masked_weights(gathered[:, :, rows, 0], lax.axis_index(axis))
    return jnp.sum(weights[:, :, None, None] * gathered[:, :, :rows], axis=0)


def entering_state(axes, decay, state):
    if len(axes) == 1:
        return entering_top(axes[0], decay, state)
    axis = axes[0]
    count = lax.axis_size(axis)
    head_total, rows, lanes = state.shape
    part = head_total // count
    packed = pack_decay(state.reshape(count, part, rows, lanes), decay.reshape(count, part))
    received = lax.all_to_all(packed, axis, 0, 0, tiled=True)
    decays = received[:, :, rows, 0]
    states = received[:, :, :rows]
    member = jnp.arange(count)
    prefixes = [
        jnp.sum(masked_weights(decays, upto)[:, :, None, None] * states, axis=0)
        for upto in range(count + 1)
    ]
    decay_before = [
        jnp.prod(jnp.where((member < upto)[:, None], decays, 1.0), axis=0)
        for upto in range(count + 1)
    ]
    group_in = entering_state(axes[1:], decay_before[count], prefixes[count])
    outgoing = jnp.stack(
        [
            decay_before[upto][:, None, None] * group_in + prefixes[upto]
            for upto in range(count)
        ]
    )
    returned = lax.all_to_all(outgoing, axis, 0, 0, tiled=True)
    return returned.reshape(head_total, rows, lanes)


def carried_state(totals, summary):
    head_total = totals.size
    state_in = entering_state(
        SEQ_AXES, totals.reshape(head_total), summary.reshape((head_total,) + summary.shape[-2:])
    )
    return state_in.reshape(summary.shape)


def per_device(
    mamba_x, gate_z, b_in, c_in, dt_raw, a_log, skip_d, norm_gain, value_weight, queries, keys
):
    tokens_here = mamba_x.shape[0]
    group_count = b_in.shape[1] // STATE
    head_count = dt_raw.shape[0]
    per_group = head_count // group_count
    inputs = mamba_x.astype(jnp.float32).reshape(tokens_here, group_count, per_group, MHEAD_DIM)
    b_group = b_in.astype(jnp.float32).reshape(tokens_here, group_count, STATE)
    c_group = c_in.astype(jnp.float32).reshape(tokens_here, group_count, STATE)
    time_step = jax.nn.softplus(dt_raw).reshape(group_count, per_group, tokens_here)
    decay_rate = jnp.exp(a_log).reshape(group_count, per_group)
    log_decay, local_out, summary, totals = block_scan(
        inputs, b_group, c_group, time_step, decay_rate
    )
    state_in = carried_state(totals, summary)
    skip_heads = skip_d.reshape(group_count, per_group)[None, :, :, None]
    ssm_out = local_out + carried_out(c_group, state_in, log_decay) + skip_heads * inputs
    mamba_out = gated_norm(ssm_out.reshape(tokens_here, -1), gate_z, norm_gain, group_count)
    kv_here = keys.shape[1] // HEAD_DIM
    per_kv = QHEADS // KVHEADS
    tp_count = lax.axis_size("tp")
    product = jnp.dot(mamba_out, value_weight, preferred_element_type=jnp.float32)
    partials = jnp.transpose(
        product.reshape(tokens_here, tp_count, kv_here * HEAD_DIM), (1, 0, 2)
    )
    exchanged = lax.all_to_all(partials, "tp", 0, 0, tiled=True)
    values = jnp.sum(exchanged, axis=0).astype(jnp.bfloat16)
    values = jnp.transpose(values.reshape(tokens_here, kv_here, HEAD_DIM), (1, 0, 2))
    key_heads = jnp.transpose(keys.reshape(tokens_here, kv_here, HEAD_DIM), (1, 0, 2))
    pair = jnp.stack([key_heads, values])
    pair = gather_by_exchange(gather_by_exchange(pair, ("zh", "zl")), "sx")
    all_pairs = jnp.transpose(pair, (2, 3, 1, 0, 4, 5)).reshape(2, kv_here, -1, HEAD_DIM)
    key_portion = all_pairs[0]
    value_portion = all_pairs[1]
    my_index = lax.axis_index(SEQ_AXES[::-1])
    query_block = query_layout(queries, kv_here, per_kv)
    query_pos = row_positions(my_index * tokens_here, tokens_here, per_kv)
    key_pos = jnp.arange(key_portion.shape[1], dtype=jnp.int32)
    scores = jnp.einsum(
        "hrd,hcd->hrc", query_block, key_portion, preferred_element_type=jnp.float32
    ) * (1.0 / math.sqrt(HEAD_DIM))
    allowed = key_pos[None, :] <= query_pos[:, None]
    scores = jnp.where(allowed[None], scores, -jnp.inf)
    row_max = jnp.max(scores, axis=2, keepdims=True)
    weights = jnp.exp(scores - row_max)
    total = jnp.sum(weights, axis=2)
    weighted = jnp.einsum(
        "hrc,hcd->hrd", weights.astype(jnp.bfloat16), value_portion, preferred_element_type=jnp.float32
    )
    attention = set_output((row_max, total, weighted), kv_here, per_kv)
    return (mamba_out, attention)


def solution(mesh):
    seq_count = mesh.shape["seq"]
    split = Mesh(
        mesh.devices.reshape(seq_count // 16, 4, 4, mesh.shape["tp"]),
        SEQ_AXES[::-1] + ("tp",),
    )
    rows = SEQ_AXES[::-1]
    placed = (
        P(rows, "tp"),
        P(rows, "tp"),
        P(rows, "tp"),
        P(rows, "tp"),
        P("tp", rows),
        P("tp"),
        P("tp"),
        P("tp"),
        P("tp", None),
        P(rows, "tp"),
        P(rows, "tp"),
    )
    return jax.shard_map(
        per_device,
        mesh=split,
        in_specs=placed,
        out_specs=(P(rows, "tp"), P(rows, "tp")),
        check_vma=False,
    )
```

```python
import math

import jax
import jax.numpy as jnp
from jax import lax
from jax.sharding import Mesh, PartitionSpec as P

MHEAD_DIM = 64
STATE = 128
QHEADS = 32
KVHEADS = 8
HEAD_DIM = 128
SEQ_AXES = (("zl", "sx"), "zh")
ROWS = ("zh", "zl", "sx")


highest = lax.Precision.HIGHEST
norm_eps = 1e-05


def block_scan(inputs, b_group, c_group, time_step, decay_rate):
    token_count = inputs.shape[0]
    log_decay = jnp.cumsum(-time_step * decay_rate[..., None], axis=2)
    log_gaps = log_decay[..., :, None] - log_decay[..., None, :]
    causal = jnp.arange(token_count)[:, None] >= jnp.arange(token_count)[None, :]
    decay_mat = jnp.exp(jnp.where(causal, log_gaps, -jnp.inf))
    cross_terms = jnp.einsum("tgn,sgn->gts", c_group, b_group, precision=highest)
    mixing = cross_terms[:, None] * decay_mat * time_step[:, :, None, :]
    local_out = jnp.einsum("gkts,sgkp->tgkp", mixing, inputs, precision=highest)
    tail_weight = jnp.exp(log_decay[..., -1:] - log_decay) * time_step
    summary = jnp.einsum("gks,sgkp,sgn->gkpn", tail_weight, inputs, b_group, precision=highest)
    return (log_decay, local_out, summary, jnp.exp(log_decay[..., -1]))


def carried_out(c_group, state_in, log_decay):
    carried_term = jnp.einsum("tgn,gkpn->tgkp", c_group, state_in, precision=highest)
    return carried_term * jnp.transpose(jnp.exp(log_decay), (2, 0, 1))[..., None]


def gated_norm(ssm_out, gate_z, norm_gain, group_count):
    token_count = ssm_out.shape[0]
    gated = ssm_out * jax.nn.silu(gate_z.astype(jnp.float32))
    grouped = gated.reshape(token_count, group_count, -1)
    inverse = lax.rsqrt(jnp.mean(grouped * grouped, axis=2, keepdims=True) + norm_eps)
    return ((grouped * inverse).reshape(token_count, -1) * norm_gain).astype(jnp.bfloat16)


def query_layout(payload, kv_here, per_kv):
    count_rows = payload.shape[0]
    shaped = payload.reshape(count_rows, kv_here, per_kv, HEAD_DIM)
    return jnp.transpose(shaped, (1, 2, 0, 3)).reshape(kv_here, per_kv * count_rows, HEAD_DIM)


def row_positions(first_pos, count_rows, per_kv):
    return jnp.tile(first_pos + jnp.arange(count_rows, dtype=jnp.int32), per_kv)


def set_output(finished_set, kv_here, per_kv):
    running_max, running_sum, running_out = finished_set
    count_rows = running_sum.shape[1] // per_kv
    result = (running_out / running_sum[..., None]).astype(jnp.bfloat16)
    result = result.reshape(kv_here, per_kv, count_rows, HEAD_DIM)
    return jnp.transpose(result, (2, 0, 1, 3)).reshape(count_rows, kv_here * per_kv * HEAD_DIM)


def gather_by_exchange(block, axis):
    count = lax.axis_size(axis)
    repeated = jnp.broadcast_to(block[None], (count,) + block.shape)
    return lax.all_to_all(repeated, axis, 0, 0, tiled=True)


def masked_weights(decays, upto):
    count = decays.shape[0]
    earlier = jnp.arange(count)[:, None]
    later = jnp.arange(count)[None, :]
    between = (later > earlier) & (later < upto)
    spans = jnp.prod(jnp.where(between[:, :, None], decays[None, :, :], 1.0), axis=1)
    return jnp.where((jnp.arange(count) < upto)[:, None], spans, 0.0)


def pack_decay(state, decay):
    extra = jnp.broadcast_to(decay[..., None, None], decay.shape + (8, state.shape[-1]))
    return jnp.concatenate([state, extra], axis=-2)


def entering_top(axis, decay, state):
    rows = state.shape[-2]
    gathered = gather_by_exchange(pack_decay(state, decay), axis)
    weights = masked_weights(gathered[:, :, rows, 0], lax.axis_index(axis))
    return jnp.sum(weights[:, :, None, None] * gathered[:, :, :rows], axis=0)


def entering_state(axes, decay, state):
    if len(axes) == 1:
        return entering_top(axes[0], decay, state)
    axis = axes[0]
    count = lax.axis_size(axis)
    head_total, rows, lanes = state.shape
    part = head_total // count
    packed = pack_decay(state.reshape(count, part, rows, lanes), decay.reshape(count, part))
    received = lax.all_to_all(packed, axis, 0, 0, tiled=True)
    decays = received[:, :, rows, 0]
    states = received[:, :, :rows]
    member = jnp.arange(count)
    bounds = jnp.arange(count + 1)
    earlier = member[None, :, None]
    between = (member[None, None, :] > member[None, :, None]) & (
        member[None, None, :] < bounds[:, None, None]
    )
    spans = jnp.prod(
        jnp.where(between[:, :, :, None], decays[None, None, :, :], 1.0), axis=2
    )
    weights = jnp.where(earlier < bounds[:, None, None], spans, 0.0)
    prefixes = jnp.sum(weights[:, :, :, None, None] * states[None], axis=1)
    decay_before = jnp.prod(
        jnp.where(earlier < bounds[:, None, None], decays[None], 1.0), axis=1
    )
    group_in = entering_state(axes[1:], decay_before[count], prefixes[count])
    outgoing = decay_before[:count, :, None, None] * group_in[None] + prefixes[:count]
    returned = lax.all_to_all(outgoing, axis, 0, 0, tiled=True)
    return returned.reshape(head_total, rows, lanes)


def carried_state(totals, summary):
    head_total = totals.size
    state_in = entering_state(
        SEQ_AXES, totals.reshape(head_total), summary.reshape((head_total,) + summary.shape[-2:])
    )
    return state_in.reshape(summary.shape)


def per_device(
    mamba_x, gate_z, b_in, c_in, dt_raw, a_log, skip_d, norm_gain, value_weight, queries, keys
):
    tokens_here = mamba_x.shape[0]
    group_count = b_in.shape[1] // STATE
    head_count = dt_raw.shape[0]
    per_group = head_count // group_count
    inputs = mamba_x.astype(jnp.float32).reshape(tokens_here, group_count, per_group, MHEAD_DIM)
    b_group = b_in.astype(jnp.float32).reshape(tokens_here, group_count, STATE)
    c_group = c_in.astype(jnp.float32).reshape(tokens_here, group_count, STATE)
    time_step = jax.nn.softplus(dt_raw).reshape(group_count, per_group, tokens_here)
    decay_rate = jnp.exp(a_log).reshape(group_count, per_group)
    log_decay, local_out, summary, totals = block_scan(
        inputs, b_group, c_group, time_step, decay_rate
    )
    state_in = carried_state(totals, summary)
    skip_heads = skip_d.reshape(group_count, per_group)[None, :, :, None]
    ssm_out = local_out + carried_out(c_group, state_in, log_decay) + skip_heads * inputs
    mamba_out = gated_norm(ssm_out.reshape(tokens_here, -1), gate_z, norm_gain, group_count)
    kv_here = keys.shape[1] // HEAD_DIM
    per_kv = QHEADS // KVHEADS
    tp_count = lax.axis_size("tp")
    product = jnp.dot(mamba_out, value_weight, preferred_element_type=jnp.float32)
    partials = jnp.transpose(
        product.reshape(tokens_here, tp_count, kv_here * HEAD_DIM), (1, 0, 2)
    )
    exchanged = lax.all_to_all(partials, "tp", 0, 0, tiled=True)
    values = jnp.sum(exchanged, axis=0).astype(jnp.bfloat16)
    values = jnp.transpose(values.reshape(tokens_here, kv_here, HEAD_DIM), (1, 0, 2))
    key_heads = jnp.transpose(keys.reshape(tokens_here, kv_here, HEAD_DIM), (1, 0, 2))
    pair = jnp.stack([key_heads, values])
    pair = gather_by_exchange(gather_by_exchange(pair, ("zh", "zl")), "sx")
    all_pairs = jnp.transpose(pair, (2, 3, 1, 0, 4, 5)).reshape(2, kv_here, -1, HEAD_DIM)
    key_portion = all_pairs[0]
    value_portion = all_pairs[1]
    my_index = lax.axis_index(ROWS)
    query_block = query_layout(queries, kv_here, per_kv)
    query_pos = row_positions(my_index * tokens_here, tokens_here, per_kv)
    key_pos = jnp.arange(key_portion.shape[1], dtype=jnp.int32)
    scores = jnp.einsum(
        "hrd,hcd->hrc", query_block, key_portion, preferred_element_type=jnp.float32
    ) * (1.0 / math.sqrt(HEAD_DIM))
    allowed = key_pos[None, :] <= query_pos[:, None]
    scores = jnp.where(allowed[None], scores, -jnp.inf)
    row_max = jnp.max(scores, axis=2, keepdims=True)
    weights = jnp.exp(scores - row_max)
    total = jnp.sum(weights, axis=2)
    weighted = jnp.einsum(
        "hrc,hcd->hrd", weights.astype(jnp.bfloat16), value_portion, preferred_element_type=jnp.float32
    )
    attention = set_output((row_max, total, weighted), kv_here, per_kv)
    return (mamba_out, attention)


def solution(mesh):
    seq_count = mesh.shape["seq"]
    split = Mesh(
        mesh.devices.reshape(seq_count // 16, 4, 4, mesh.shape["tp"]),
        ROWS + ("tp",),
    )
    rows = ROWS
    placed = (
        P(rows, "tp"),
        P(rows, "tp"),
        P(rows, "tp"),
        P(rows, "tp"),
        P("tp", rows),
        P("tp"),
        P("tp"),
        P("tp"),
        P("tp", None),
        P(rows, "tp"),
        P(rows, "tp"),
    )
    return jax.shard_map(
        per_device,
        mesh=split,
        in_specs=placed,
        out_specs=(P(rows, "tp"), P(rows, "tp")),
        check_vma=False,
    )
```

```python
import math

import jax
import jax.numpy as jnp
from jax import lax
from jax.sharding import Mesh, PartitionSpec as P

MHEAD_DIM = 64
STATE = 128
QHEADS = 32
KVHEADS = 8
HEAD_DIM = 128
SEQ_AXES = (("zl", "sx"), "zh")
ROWS = ("zh", "zl", "sx")


highest = lax.Precision.HIGHEST
norm_eps = 1e-05


def block_scan(inputs, b_group, c_group, time_step, decay_rate):
    token_count = inputs.shape[0]
    log_decay = jnp.cumsum(-time_step * decay_rate[..., None], axis=2)
    log_gaps = log_decay[..., :, None] - log_decay[..., None, :]
    causal = jnp.arange(token_count)[:, None] >= jnp.arange(token_count)[None, :]
    decay_mat = jnp.exp(jnp.where(causal, log_gaps, -jnp.inf))
    cross_terms = jnp.einsum("tgn,sgn->gts", c_group, b_group, precision=highest)
    mixing = cross_terms[:, None] * decay_mat * time_step[:, :, None, :]
    local_out = jnp.einsum("gkts,sgkp->tgkp", mixing, inputs, precision=highest)
    tail_weight = jnp.exp(log_decay[..., -1:] - log_decay) * time_step
    summary = jnp.einsum("gks,sgkp,sgn->gkpn", tail_weight, inputs, b_group, precision=highest)
    return (log_decay, local_out, summary, jnp.exp(log_decay[..., -1]))


def carried_out(c_group, state_in, log_decay):
    carried_term = jnp.einsum("tgn,gkpn->tgkp", c_group, state_in, precision=highest)
    return carried_term * jnp.transpose(jnp.exp(log_decay), (2, 0, 1))[..., None]


def gated_norm(ssm_out, gate_z, norm_gain, group_count):
    token_count = ssm_out.shape[0]
    gated = ssm_out * jax.nn.silu(gate_z.astype(jnp.float32))
    grouped = gated.reshape(token_count, group_count, -1)
    inverse = lax.rsqrt(jnp.mean(grouped * grouped, axis=2, keepdims=True) + norm_eps)
    return ((grouped * inverse).reshape(token_count, -1) * norm_gain).astype(jnp.bfloat16)


def query_layout(payload, kv_here, per_kv):
    count_rows = payload.shape[0]
    shaped = payload.reshape(count_rows, kv_here, per_kv, HEAD_DIM)
    return jnp.transpose(shaped, (1, 2, 0, 3)).reshape(kv_here, per_kv * count_rows, HEAD_DIM)


def row_positions(first_pos, count_rows, per_kv):
    return jnp.tile(first_pos + jnp.arange(count_rows, dtype=jnp.int32), per_kv)


def set_output(finished_set, kv_here, per_kv):
    running_max, running_sum, running_out = finished_set
    count_rows = running_sum.shape[1] // per_kv
    result = (running_out / running_sum[..., None]).astype(jnp.bfloat16)
    result = result.reshape(kv_here, per_kv, count_rows, HEAD_DIM)
    return jnp.transpose(result, (2, 0, 1, 3)).reshape(count_rows, kv_here * per_kv * HEAD_DIM)


def gather_by_exchange(block, axis):
    count = lax.axis_size(axis)
    repeated = jnp.broadcast_to(block[None], (count,) + block.shape)
    return lax.all_to_all(repeated, axis, 0, 0, tiled=True)


def gather_around(block, axis):
    count = lax.axis_size(axis)
    here = lax.axis_index(axis)
    shifted = [block]
    for shift in range(1, count):
        pairs = [(source, (source + shift) % count) for source in range(count)]
        shifted.append(lax.ppermute(block, axis, pairs))
    stacked = jnp.stack(shifted)
    return stacked[(here - jnp.arange(count)) % count]


def masked_weights(decays, upto):
    count = decays.shape[0]
    earlier = jnp.arange(count)[:, None]
    later = jnp.arange(count)[None, :]
    between = (later > earlier) & (later < upto)
    spans = jnp.prod(jnp.where(between[:, :, None], decays[None, :, :], 1.0), axis=1)
    return jnp.where((jnp.arange(count) < upto)[:, None], spans, 0.0)


def pack_decay(state, decay):
    extra = jnp.broadcast_to(decay[..., None, None], decay.shape + (8, state.shape[-1]))
    return jnp.concatenate([state, extra], axis=-2)


def entering_top(axis, decay, state):
    rows = state.shape[-2]
    gathered = gather_by_exchange(pack_decay(state, decay), axis)
    weights = masked_weights(gathered[:, :, rows, 0], lax.axis_index(axis))
    return jnp.sum(weights[:, :, None, None] * gathered[:, :, :rows], axis=0)


def entering_state(axes, decay, state):
    if len(axes) == 1:
        return entering_top(axes[0], decay, state)
    axis = axes[0]
    count = lax.axis_size(axis)
    head_total, rows, lanes = state.shape
    part = head_total // count
    packed = pack_decay(state.reshape(count, part, rows, lanes), decay.reshape(count, part))
    received = lax.all_to_all(packed, axis, 0, 0, tiled=True)
    decays = received[:, :, rows, 0]
    states = received[:, :, :rows]
    member = jnp.arange(count)
    bounds = jnp.arange(count + 1)
    earlier = member[None, :, None]
    between = (member[None, None, :] > member[None, :, None]) & (
        member[None, None, :] < bounds[:, None, None]
    )
    spans = jnp.prod(
        jnp.where(between[:, :, :, None], decays[None, None, :, :], 1.0), axis=2
    )
    weights = jnp.where(earlier < bounds[:, None, None], spans, 0.0)
    prefixes = jnp.sum(weights[:, :, :, None, None] * states[None], axis=1)
    decay_before = jnp.prod(
        jnp.where(earlier < bounds[:, None, None], decays[None], 1.0), axis=1
    )
    group_in = entering_state(axes[1:], decay_before[count], prefixes[count])
    outgoing = decay_before[:count, :, None, None] * group_in[None] + prefixes[:count]
    returned = lax.all_to_all(outgoing, axis, 0, 0, tiled=True)
    return returned.reshape(head_total, rows, lanes)


def carried_state(totals, summary):
    head_total = totals.size
    state_in = entering_state(
        SEQ_AXES, totals.reshape(head_total), summary.reshape((head_total,) + summary.shape[-2:])
    )
    return state_in.reshape(summary.shape)


def per_device(
    mamba_x, gate_z, b_in, c_in, dt_raw, a_log, skip_d, norm_gain, value_weight, queries, keys
):
    tokens_here = mamba_x.shape[0]
    group_count = b_in.shape[1] // STATE
    head_count = dt_raw.shape[0]
    per_group = head_count // group_count
    inputs = mamba_x.astype(jnp.float32).reshape(tokens_here, group_count, per_group, MHEAD_DIM)
    b_group = b_in.astype(jnp.float32).reshape(tokens_here, group_count, STATE)
    c_group = c_in.astype(jnp.float32).reshape(tokens_here, group_count, STATE)
    time_step = jax.nn.softplus(dt_raw).reshape(group_count, per_group, tokens_here)
    decay_rate = jnp.exp(a_log).reshape(group_count, per_group)
    log_decay, local_out, summary, totals = block_scan(
        inputs, b_group, c_group, time_step, decay_rate
    )
    state_in = carried_state(totals, summary)
    skip_heads = skip_d.reshape(group_count, per_group)[None, :, :, None]
    ssm_out = local_out + carried_out(c_group, state_in, log_decay) + skip_heads * inputs
    mamba_out = gated_norm(ssm_out.reshape(tokens_here, -1), gate_z, norm_gain, group_count)
    kv_here = keys.shape[1] // HEAD_DIM
    per_kv = QHEADS // KVHEADS
    tp_count = lax.axis_size("tp")
    product = jnp.dot(mamba_out, value_weight, preferred_element_type=jnp.float32)
    partials = jnp.transpose(
        product.reshape(tokens_here, tp_count, kv_here * HEAD_DIM), (1, 0, 2)
    )
    exchanged = lax.all_to_all(partials, "tp", 0, 0, tiled=True)
    values = jnp.sum(exchanged, axis=0).astype(jnp.bfloat16)
    values = jnp.transpose(values.reshape(tokens_here, kv_here, HEAD_DIM), (1, 0, 2))
    key_heads = jnp.transpose(keys.reshape(tokens_here, kv_here, HEAD_DIM), (1, 0, 2))
    pair = jnp.stack([key_heads, values])
    pair = gather_around(gather_by_exchange(pair, ("zh", "zl")), "sx")
    all_pairs = jnp.transpose(pair, (2, 3, 1, 0, 4, 5)).reshape(2, kv_here, -1, HEAD_DIM)
    key_portion = all_pairs[0]
    value_portion = all_pairs[1]
    my_index = lax.axis_index(ROWS)
    query_block = query_layout(queries, kv_here, per_kv)
    query_pos = row_positions(my_index * tokens_here, tokens_here, per_kv)
    key_pos = jnp.arange(key_portion.shape[1], dtype=jnp.int32)
    scores = jnp.einsum(
        "hrd,hcd->hrc", query_block, key_portion, preferred_element_type=jnp.float32
    ) * (1.0 / math.sqrt(HEAD_DIM))
    allowed = key_pos[None, :] <= query_pos[:, None]
    scores = jnp.where(allowed[None], scores, -jnp.inf)
    row_max = jnp.max(scores, axis=2, keepdims=True)
    weights = jnp.exp(scores - row_max)
    total = jnp.sum(weights, axis=2)
    weighted = jnp.einsum(
        "hrc,hcd->hrd", weights.astype(jnp.bfloat16), value_portion, preferred_element_type=jnp.float32
    )
    attention = set_output((row_max, total, weighted), kv_here, per_kv)
    return (mamba_out, attention)


def solution(mesh):
    seq_count = mesh.shape["seq"]
    split = Mesh(
        mesh.devices.reshape(seq_count // 16, 4, 4, mesh.shape["tp"]),
        ROWS + ("tp",),
    )
    rows = ROWS
    placed = (
        P(rows, "tp"),
        P(rows, "tp"),
        P(rows, "tp"),
        P(rows, "tp"),
        P("tp", rows),
        P("tp"),
        P("tp"),
        P("tp"),
        P("tp", None),
        P(rows, "tp"),
        P(rows, "tp"),
    )
    return jax.shard_map(
        per_device,
        mesh=split,
        in_specs=placed,
        out_specs=(P(rows, "tp"), P(rows, "tp")),
        check_vma=False,
    )
```

```python
import math

import jax
import jax.numpy as jnp
from jax import lax
from jax.sharding import Mesh, PartitionSpec as P

MHEAD_DIM = 64
STATE = 128
QHEADS = 32
KVHEADS = 8
HEAD_DIM = 128
SEQ_AXES = (("zl", "sx"), "zh")
ROWS = ("zh", "zl", "sx")


highest = lax.Precision.HIGHEST
norm_eps = 1e-05


def block_scan(inputs, b_group, c_group, time_step, decay_rate):
    token_count = inputs.shape[0]
    log_decay = jnp.cumsum(-time_step * decay_rate[..., None], axis=2)
    log_gaps = log_decay[..., :, None] - log_decay[..., None, :]
    causal = jnp.arange(token_count)[:, None] >= jnp.arange(token_count)[None, :]
    decay_mat = jnp.exp(jnp.where(causal, log_gaps, -jnp.inf))
    cross_terms = jnp.einsum("tgn,sgn->gts", c_group, b_group, precision=highest)
    mixing = cross_terms[:, None] * decay_mat * time_step[:, :, None, :]
    local_out = jnp.einsum("gkts,sgkp->tgkp", mixing, inputs, precision=highest)
    tail_weight = jnp.exp(log_decay[..., -1:] - log_decay) * time_step
    summary = jnp.einsum("gks,sgkp,sgn->gkpn", tail_weight, inputs, b_group, precision=highest)
    return (log_decay, local_out, summary, jnp.exp(log_decay[..., -1]))


def carried_out(c_group, state_in, log_decay):
    carried_term = jnp.einsum("tgn,gkpn->tgkp", c_group, state_in, precision=highest)
    return carried_term * jnp.transpose(jnp.exp(log_decay), (2, 0, 1))[..., None]


def gated_norm(ssm_out, gate_z, norm_gain, group_count):
    token_count = ssm_out.shape[0]
    gated = ssm_out * jax.nn.silu(gate_z.astype(jnp.float32))
    grouped = gated.reshape(token_count, group_count, -1)
    inverse = lax.rsqrt(jnp.mean(grouped * grouped, axis=2, keepdims=True) + norm_eps)
    return ((grouped * inverse).reshape(token_count, -1) * norm_gain).astype(jnp.bfloat16)


def query_layout(payload, kv_here, per_kv):
    count_rows = payload.shape[0]
    shaped = payload.reshape(count_rows, kv_here, per_kv, HEAD_DIM)
    return jnp.transpose(shaped, (1, 2, 0, 3)).reshape(kv_here, per_kv * count_rows, HEAD_DIM)


def row_positions(first_pos, count_rows, per_kv):
    return jnp.tile(first_pos + jnp.arange(count_rows, dtype=jnp.int32), per_kv)


def set_output(finished_set, kv_here, per_kv):
    running_max, running_sum, running_out = finished_set
    count_rows = running_sum.shape[1] // per_kv
    result = (running_out / running_sum[..., None]).astype(jnp.bfloat16)
    result = result.reshape(kv_here, per_kv, count_rows, HEAD_DIM)
    return jnp.transpose(result, (2, 0, 1, 3)).reshape(count_rows, kv_here * per_kv * HEAD_DIM)


def gather_by_exchange(block, axis):
    count = lax.axis_size(axis)
    repeated = jnp.broadcast_to(block[None], (count,) + block.shape)
    return lax.all_to_all(repeated, axis, 0, 0, tiled=True)


def masked_weights(decays, upto):
    count = decays.shape[0]
    earlier = jnp.arange(count)[:, None]
    later = jnp.arange(count)[None, :]
    between = (later > earlier) & (later < upto)
    spans = jnp.prod(jnp.where(between[:, :, None], decays[None, :, :], 1.0), axis=1)
    return jnp.where((jnp.arange(count) < upto)[:, None], spans, 0.0)


def pack_decay(state, decay):
    extra = jnp.broadcast_to(decay[..., None, None], decay.shape + (8, state.shape[-1]))
    return jnp.concatenate([state, extra], axis=-2)


def entering_top(axis, decay, state):
    rows = state.shape[-2]
    gathered = gather_by_exchange(pack_decay(state, decay), axis)
    weights = masked_weights(gathered[:, :, rows, 0], lax.axis_index(axis))
    return jnp.sum(weights[:, :, None, None] * gathered[:, :, :rows], axis=0)


def entering_state(axes, decay, state):
    if len(axes) == 1:
        return entering_top(axes[0], decay, state)
    axis = axes[0]
    count = lax.axis_size(axis)
    head_total, rows, lanes = state.shape
    part = head_total // count
    packed = pack_decay(state.reshape(count, part, rows, lanes), decay.reshape(count, part))
    received = lax.all_to_all(packed, axis, 0, 0, tiled=True)
    decays = received[:, :, rows, 0]
    states = received[:, :, :rows]
    member = jnp.arange(count)
    bounds = jnp.arange(count + 1)
    earlier = member[None, :, None]
    between = (member[None, None, :] > member[None, :, None]) & (
        member[None, None, :] < bounds[:, None, None]
    )
    spans = jnp.prod(
        jnp.where(between[:, :, :, None], decays[None, None, :, :], 1.0), axis=2
    )
    weights = jnp.where(earlier < bounds[:, None, None], spans, 0.0)
    prefixes = jnp.sum(weights[:, :, :, None, None] * states[None], axis=1)
    decay_before = jnp.prod(
        jnp.where(earlier < bounds[:, None, None], decays[None], 1.0), axis=1
    )
    group_in = entering_state(axes[1:], decay_before[count], prefixes[count])
    outgoing = decay_before[:count, :, None, None] * group_in[None] + prefixes[:count]
    returned = lax.all_to_all(outgoing, axis, 0, 0, tiled=True)
    return returned.reshape(head_total, rows, lanes)


def carried_state(totals, summary):
    head_total = totals.size
    state_in = entering_state(
        SEQ_AXES, totals.reshape(head_total), summary.reshape((head_total,) + summary.shape[-2:])
    )
    return state_in.reshape(summary.shape)


def per_device(
    mamba_x, gate_z, b_in, c_in, dt_raw, a_log, skip_d, norm_gain, value_weight, queries, keys
):
    tokens_here = mamba_x.shape[0]
    group_count = b_in.shape[1] // STATE
    head_count = dt_raw.shape[0]
    per_group = head_count // group_count
    inputs = mamba_x.astype(jnp.float32).reshape(tokens_here, group_count, per_group, MHEAD_DIM)
    b_group = b_in.astype(jnp.float32).reshape(tokens_here, group_count, STATE)
    c_group = c_in.astype(jnp.float32).reshape(tokens_here, group_count, STATE)
    time_step = jax.nn.softplus(dt_raw).reshape(group_count, per_group, tokens_here)
    decay_rate = jnp.exp(a_log).reshape(group_count, per_group)
    log_decay, local_out, summary, totals = block_scan(
        inputs, b_group, c_group, time_step, decay_rate
    )
    state_in = carried_state(totals, summary)
    skip_heads = skip_d.reshape(group_count, per_group)[None, :, :, None]
    ssm_out = local_out + carried_out(c_group, state_in, log_decay) + skip_heads * inputs
    mamba_out = gated_norm(ssm_out.reshape(tokens_here, -1), gate_z, norm_gain, group_count)
    kv_here = keys.shape[1] // HEAD_DIM
    per_kv = QHEADS // KVHEADS
    tp_count = lax.axis_size("tp")
    product = jnp.dot(mamba_out, value_weight, preferred_element_type=jnp.float32)
    partials = jnp.transpose(
        product.reshape(tokens_here, tp_count, kv_here * HEAD_DIM), (1, 0, 2)
    )
    exchanged = lax.all_to_all(partials, "tp", 0, 0, tiled=True)
    values = jnp.sum(exchanged, axis=0).astype(jnp.bfloat16)
    values = jnp.transpose(values.reshape(tokens_here, kv_here, HEAD_DIM), (1, 0, 2))
    key_heads = jnp.transpose(keys.reshape(tokens_here, kv_here, HEAD_DIM), (1, 0, 2))
    pair = jnp.stack([key_heads, values])
    pair = gather_by_exchange(lax.all_gather(pair, ("zh", "zl")), "sx")
    all_pairs = jnp.transpose(pair, (2, 3, 1, 0, 4, 5)).reshape(2, kv_here, -1, HEAD_DIM)
    key_portion = all_pairs[0]
    value_portion = all_pairs[1]
    my_index = lax.axis_index(ROWS)
    query_block = query_layout(queries, kv_here, per_kv)
    query_pos = row_positions(my_index * tokens_here, tokens_here, per_kv)
    key_pos = jnp.arange(key_portion.shape[1], dtype=jnp.int32)
    scores = jnp.einsum(
        "hrd,hcd->hrc", query_block, key_portion, preferred_element_type=jnp.float32
    ) * (1.0 / math.sqrt(HEAD_DIM))
    allowed = key_pos[None, :] <= query_pos[:, None]
    scores = jnp.where(allowed[None], scores, -jnp.inf)
    row_max = jnp.max(scores, axis=2, keepdims=True)
    weights = jnp.exp(scores - row_max)
    total = jnp.sum(weights, axis=2)
    weighted = jnp.einsum(
        "hrc,hcd->hrd", weights.astype(jnp.bfloat16), value_portion, preferred_element_type=jnp.float32
    )
    attention = set_output((row_max, total, weighted), kv_here, per_kv)
    return (mamba_out, attention)


def solution(mesh):
    seq_count = mesh.shape["seq"]
    split = Mesh(
        mesh.devices.reshape(seq_count // 16, 4, 4, mesh.shape["tp"]),
        ROWS + ("tp",),
    )
    rows = ROWS
    placed = (
        P(rows, "tp"),
        P(rows, "tp"),
        P(rows, "tp"),
        P(rows, "tp"),
        P("tp", rows),
        P("tp"),
        P("tp"),
        P("tp"),
        P("tp", None),
        P(rows, "tp"),
        P(rows, "tp"),
    )
    return jax.shard_map(
        per_device,
        mesh=split,
        in_specs=placed,
        out_specs=(P(rows, "tp"), P(rows, "tp")),
        check_vma=False,
    )
```

```python
import math

import jax
import jax.numpy as jnp
from jax import lax
from jax.sharding import Mesh, PartitionSpec as P

MHEAD_DIM = 64
STATE = 128
QHEADS = 32
KVHEADS = 8
HEAD_DIM = 128
SEQ_AXES = (("zl", "sx"), "zh")
ROWS = ("zh", "zl", "sx")


highest = lax.Precision.HIGHEST
norm_eps = 1e-05


def block_scan(inputs, b_group, c_group, time_step, decay_rate):
    token_count = inputs.shape[0]
    log_decay = jnp.cumsum(-time_step * decay_rate[..., None], axis=2)
    log_gaps = log_decay[..., :, None] - log_decay[..., None, :]
    causal = jnp.arange(token_count)[:, None] >= jnp.arange(token_count)[None, :]
    decay_mat = jnp.exp(jnp.where(causal, log_gaps, -jnp.inf))
    cross_terms = jnp.einsum("tgn,sgn->gts", c_group, b_group, precision=highest)
    mixing = cross_terms[:, None] * decay_mat * time_step[:, :, None, :]
    local_out = jnp.einsum("gkts,sgkp->tgkp", mixing, inputs, precision=highest)
    tail_weight = jnp.exp(log_decay[..., -1:] - log_decay) * time_step
    summary = jnp.einsum("gks,sgkp,sgn->gkpn", tail_weight, inputs, b_group, precision=highest)
    return (log_decay, local_out, summary, jnp.exp(log_decay[..., -1]))


def carried_out(c_group, state_in, log_decay):
    carried_term = jnp.einsum("tgn,gkpn->tgkp", c_group, state_in, precision=highest)
    return carried_term * jnp.transpose(jnp.exp(log_decay), (2, 0, 1))[..., None]


def gated_norm(ssm_out, gate_z, norm_gain, group_count):
    token_count = ssm_out.shape[0]
    gated = ssm_out * jax.nn.silu(gate_z.astype(jnp.float32))
    grouped = gated.reshape(token_count, group_count, -1)
    inverse = lax.rsqrt(jnp.mean(grouped * grouped, axis=2, keepdims=True) + norm_eps)
    return ((grouped * inverse).reshape(token_count, -1) * norm_gain).astype(jnp.bfloat16)


def query_layout(payload, kv_here, per_kv):
    count_rows = payload.shape[0]
    shaped = payload.reshape(count_rows, kv_here, per_kv, HEAD_DIM)
    return jnp.transpose(shaped, (1, 2, 0, 3)).reshape(kv_here, per_kv * count_rows, HEAD_DIM)


def row_positions(first_pos, count_rows, per_kv):
    return jnp.tile(first_pos + jnp.arange(count_rows, dtype=jnp.int32), per_kv)


def set_output(finished_set, kv_here, per_kv):
    running_max, running_sum, running_out = finished_set
    count_rows = running_sum.shape[1] // per_kv
    result = (running_out / running_sum[..., None]).astype(jnp.bfloat16)
    result = result.reshape(kv_here, per_kv, count_rows, HEAD_DIM)
    return jnp.transpose(result, (2, 0, 1, 3)).reshape(count_rows, kv_here * per_kv * HEAD_DIM)


def gather_by_exchange(block, axis):
    count = lax.axis_size(axis)
    repeated = jnp.broadcast_to(block[None], (count,) + block.shape)
    return lax.all_to_all(repeated, axis, 0, 0, tiled=True)


def masked_weights(decays, upto):
    count = decays.shape[0]
    earlier = jnp.arange(count)[:, None]
    later = jnp.arange(count)[None, :]
    between = (later > earlier) & (later < upto)
    spans = jnp.prod(jnp.where(between[:, :, None], decays[None, :, :], 1.0), axis=1)
    return jnp.where((jnp.arange(count) < upto)[:, None], spans, 0.0)


def pack_decay(state, decay):
    extra = jnp.broadcast_to(decay[..., None, None], decay.shape + (8, state.shape[-1]))
    return jnp.concatenate([state, extra], axis=-2)


def entering_top(axis, decay, state):
    rows = state.shape[-2]
    gathered = lax.all_gather(pack_decay(state, decay), axis)
    weights = masked_weights(gathered[:, :, rows, 0], lax.axis_index(axis))
    return jnp.sum(weights[:, :, None, None] * gathered[:, :, :rows], axis=0)


def entering_state(axes, decay, state):
    if len(axes) == 1:
        return entering_top(axes[0], decay, state)
    axis = axes[0]
    count = lax.axis_size(axis)
    head_total, rows, lanes = state.shape
    part = head_total // count
    packed = pack_decay(state.reshape(count, part, rows, lanes), decay.reshape(count, part))
    received = lax.all_to_all(packed, axis, 0, 0, tiled=True)
    decays = received[:, :, rows, 0]
    states = received[:, :, :rows]
    member = jnp.arange(count)
    bounds = jnp.arange(count + 1)
    earlier = member[None, :, None]
    between = (member[None, None, :] > member[None, :, None]) & (
        member[None, None, :] < bounds[:, None, None]
    )
    spans = jnp.prod(
        jnp.where(between[:, :, :, None], decays[None, None, :, :], 1.0), axis=2
    )
    weights = jnp.where(earlier < bounds[:, None, None], spans, 0.0)
    prefixes = jnp.sum(weights[:, :, :, None, None] * states[None], axis=1)
    decay_before = jnp.prod(
        jnp.where(earlier < bounds[:, None, None], decays[None], 1.0), axis=1
    )
    group_in = entering_state(axes[1:], decay_before[count], prefixes[count])
    outgoing = decay_before[:count, :, None, None] * group_in[None] + prefixes[:count]
    returned = lax.all_to_all(outgoing, axis, 0, 0, tiled=True)
    return returned.reshape(head_total, rows, lanes)


def carried_state(totals, summary):
    head_total = totals.size
    state_in = entering_state(
        SEQ_AXES, totals.reshape(head_total), summary.reshape((head_total,) + summary.shape[-2:])
    )
    return state_in.reshape(summary.shape)


def per_device(
    mamba_x, gate_z, b_in, c_in, dt_raw, a_log, skip_d, norm_gain, value_weight, queries, keys
):
    tokens_here = mamba_x.shape[0]
    group_count = b_in.shape[1] // STATE
    head_count = dt_raw.shape[0]
    per_group = head_count // group_count
    inputs = mamba_x.astype(jnp.float32).reshape(tokens_here, group_count, per_group, MHEAD_DIM)
    b_group = b_in.astype(jnp.float32).reshape(tokens_here, group_count, STATE)
    c_group = c_in.astype(jnp.float32).reshape(tokens_here, group_count, STATE)
    time_step = jax.nn.softplus(dt_raw).reshape(group_count, per_group, tokens_here)
    decay_rate = jnp.exp(a_log).reshape(group_count, per_group)
    log_decay, local_out, summary, totals = block_scan(
        inputs, b_group, c_group, time_step, decay_rate
    )
    state_in = carried_state(totals, summary)
    skip_heads = skip_d.reshape(group_count, per_group)[None, :, :, None]
    ssm_out = local_out + carried_out(c_group, state_in, log_decay) + skip_heads * inputs
    mamba_out = gated_norm(ssm_out.reshape(tokens_here, -1), gate_z, norm_gain, group_count)
    kv_here = keys.shape[1] // HEAD_DIM
    per_kv = QHEADS // KVHEADS
    tp_count = lax.axis_size("tp")
    product = jnp.dot(mamba_out, value_weight, preferred_element_type=jnp.float32)
    partials = jnp.transpose(
        product.reshape(tokens_here, tp_count, kv_here * HEAD_DIM), (1, 0, 2)
    )
    exchanged = lax.all_to_all(partials, "tp", 0, 0, tiled=True)
    values = jnp.sum(exchanged, axis=0).astype(jnp.bfloat16)
    values = jnp.transpose(values.reshape(tokens_here, kv_here, HEAD_DIM), (1, 0, 2))
    key_heads = jnp.transpose(keys.reshape(tokens_here, kv_here, HEAD_DIM), (1, 0, 2))
    pair = jnp.stack([key_heads, values])
    pair = gather_by_exchange(lax.all_gather(pair, ("zh", "zl")), "sx")
    all_pairs = jnp.transpose(pair, (2, 3, 1, 0, 4, 5)).reshape(2, kv_here, -1, HEAD_DIM)
    key_portion = all_pairs[0]
    value_portion = all_pairs[1]
    my_index = lax.axis_index(ROWS)
    query_block = query_layout(queries, kv_here, per_kv)
    query_pos = row_positions(my_index * tokens_here, tokens_here, per_kv)
    key_pos = jnp.arange(key_portion.shape[1], dtype=jnp.int32)
    scores = jnp.einsum(
        "hrd,hcd->hrc", query_block, key_portion, preferred_element_type=jnp.float32
    ) * (1.0 / math.sqrt(HEAD_DIM))
    allowed = key_pos[None, :] <= query_pos[:, None]
    scores = jnp.where(allowed[None], scores, -jnp.inf)
    row_max = jnp.max(scores, axis=2, keepdims=True)
    weights = jnp.exp(scores - row_max)
    total = jnp.sum(weights, axis=2)
    weighted = jnp.einsum(
        "hrc,hcd->hrd", weights.astype(jnp.bfloat16), value_portion, preferred_element_type=jnp.float32
    )
    attention = set_output((row_max, total, weighted), kv_here, per_kv)
    return (mamba_out, attention)


def solution(mesh):
    seq_count = mesh.shape["seq"]
    split = Mesh(
        mesh.devices.reshape(seq_count // 16, 4, 4, mesh.shape["tp"]),
        ROWS + ("tp",),
    )
    rows = ROWS
    placed = (
        P(rows, "tp"),
        P(rows, "tp"),
        P(rows, "tp"),
        P(rows, "tp"),
        P("tp", rows),
        P("tp"),
        P("tp"),
        P("tp"),
        P("tp", None),
        P(rows, "tp"),
        P(rows, "tp"),
    )
    return jax.shard_map(
        per_device,
        mesh=split,
        in_specs=placed,
        out_specs=(P(rows, "tp"), P(rows, "tp")),
        check_vma=False,
    )
```

```python
import math

import jax
import jax.numpy as jnp
from jax import lax
from jax.sharding import Mesh, PartitionSpec as P

MHEAD_DIM = 64
STATE = 128
QHEADS = 32
KVHEADS = 8
HEAD_DIM = 128
SEQ_AXES = (("zl", "sx"), "zh")
ROWS = ("zh", "zl", "sx")


highest = lax.Precision.HIGHEST
norm_eps = 1e-05


def block_scan(inputs, b_group, c_group, time_step, decay_rate):
    token_count = inputs.shape[0]
    log_decay = jnp.cumsum(-time_step * decay_rate[..., None], axis=2)
    log_gaps = log_decay[..., :, None] - log_decay[..., None, :]
    causal = jnp.arange(token_count)[:, None] >= jnp.arange(token_count)[None, :]
    decay_mat = jnp.exp(jnp.where(causal, log_gaps, -jnp.inf))
    cross_terms = jnp.einsum("tgn,sgn->gts", c_group, b_group, precision=highest)
    mixing = cross_terms[:, None] * decay_mat * time_step[:, :, None, :]
    local_out = jnp.einsum("gkts,sgkp->tgkp", mixing, inputs, precision=highest)
    tail_weight = jnp.exp(log_decay[..., -1:] - log_decay) * time_step
    summary = jnp.einsum("gks,sgkp,sgn->gkpn", tail_weight, inputs, b_group, precision=highest)
    return (log_decay, local_out, summary, jnp.exp(log_decay[..., -1]))


def carried_out(c_group, state_in, log_decay):
    carried_term = jnp.einsum("tgn,gkpn->tgkp", c_group, state_in, precision=highest)
    return carried_term * jnp.transpose(jnp.exp(log_decay), (2, 0, 1))[..., None]


def gated_norm(ssm_out, gate_z, norm_gain, group_count):
    token_count = ssm_out.shape[0]
    gated = ssm_out * jax.nn.silu(gate_z.astype(jnp.float32))
    grouped = gated.reshape(token_count, group_count, -1)
    inverse = lax.rsqrt(jnp.mean(grouped * grouped, axis=2, keepdims=True) + norm_eps)
    return ((grouped * inverse).reshape(token_count, -1) * norm_gain).astype(jnp.bfloat16)


def query_layout(payload, kv_here, per_kv):
    count_rows = payload.shape[0]
    shaped = payload.reshape(count_rows, kv_here, per_kv, HEAD_DIM)
    return jnp.transpose(shaped, (1, 2, 0, 3)).reshape(kv_here, per_kv * count_rows, HEAD_DIM)


def row_positions(first_pos, count_rows, per_kv):
    return jnp.tile(first_pos + jnp.arange(count_rows, dtype=jnp.int32), per_kv)


def set_output(finished_set, kv_here, per_kv):
    running_max, running_sum, running_out = finished_set
    count_rows = running_sum.shape[1] // per_kv
    result = (running_out / running_sum[..., None]).astype(jnp.bfloat16)
    result = result.reshape(kv_here, per_kv, count_rows, HEAD_DIM)
    return jnp.transpose(result, (2, 0, 1, 3)).reshape(count_rows, kv_here * per_kv * HEAD_DIM)


def gather_by_exchange(block, axis):
    count = lax.axis_size(axis)
    repeated = jnp.broadcast_to(block[None], (count,) + block.shape)
    return lax.all_to_all(repeated, axis, 0, 0, tiled=True)


def gather_earlier(block, axis):
    count = lax.axis_size(axis)
    here = lax.axis_index(axis)
    shifted = [block]
    for shift in range(1, count):
        pairs = [(source, source + shift) for source in range(count - shift)]
        shifted.append(lax.ppermute(block, axis, pairs))
    return jnp.stack(shifted)


def masked_weights(decays, upto):
    count = decays.shape[0]
    earlier = jnp.arange(count)[:, None]
    later = jnp.arange(count)[None, :]
    between = (later > earlier) & (later < upto)
    spans = jnp.prod(jnp.where(between[:, :, None], decays[None, :, :], 1.0), axis=1)
    return jnp.where((jnp.arange(count) < upto)[:, None], spans, 0.0)


def pack_decay(state, decay):
    extra = jnp.broadcast_to(decay[..., None, None], decay.shape + (8, state.shape[-1]))
    return jnp.concatenate([state, extra], axis=-2)


def entering_top(axis, decay, state):
    rows = state.shape[-2]
    shifted = gather_earlier(pack_decay(state, decay), axis)
    here = lax.axis_index(axis)
    count = shifted.shape[0]
    decays = shifted[:, :, rows, 0]
    present = (jnp.arange(count) >= 1) & (jnp.arange(count) <= here)
    carried = jnp.where(present[:, None], decays, 1.0)
    spans = jnp.cumprod(jnp.concatenate([jnp.ones_like(carried[:1]), carried[:-1]]), axis=0)
    weights = jnp.where(present[:, None], spans, 0.0)
    return jnp.sum(weights[:, :, None, None] * shifted[:, :, :rows], axis=0)


def entering_state(axes, decay, state):
    if len(axes) == 1:
        return entering_top(axes[0], decay, state)
    axis = axes[0]
    count = lax.axis_size(axis)
    head_total, rows, lanes = state.shape
    part = head_total // count
    packed = pack_decay(state.reshape(count, part, rows, lanes), decay.reshape(count, part))
    received = lax.all_to_all(packed, axis, 0, 0, tiled=True)
    decays = received[:, :, rows, 0]
    states = received[:, :, :rows]
    member = jnp.arange(count)
    bounds = jnp.arange(count + 1)
    earlier = member[None, :, None]
    between = (member[None, None, :] > member[None, :, None]) & (
        member[None, None, :] < bounds[:, None, None]
    )
    spans = jnp.prod(
        jnp.where(between[:, :, :, None], decays[None, None, :, :], 1.0), axis=2
    )
    weights = jnp.where(earlier < bounds[:, None, None], spans, 0.0)
    prefixes = jnp.sum(weights[:, :, :, None, None] * states[None], axis=1)
    decay_before = jnp.prod(
        jnp.where(earlier < bounds[:, None, None], decays[None], 1.0), axis=1
    )
    group_in = entering_state(axes[1:], decay_before[count], prefixes[count])
    outgoing = decay_before[:count, :, None, None] * group_in[None] + prefixes[:count]
    returned = lax.all_to_all(outgoing, axis, 0, 0, tiled=True)
    return returned.reshape(head_total, rows, lanes)


def carried_state(totals, summary):
    head_total = totals.size
    state_in = entering_state(
        SEQ_AXES, totals.reshape(head_total), summary.reshape((head_total,) + summary.shape[-2:])
    )
    return state_in.reshape(summary.shape)


def per_device(
    mamba_x, gate_z, b_in, c_in, dt_raw, a_log, skip_d, norm_gain, value_weight, queries, keys
):
    tokens_here = mamba_x.shape[0]
    group_count = b_in.shape[1] // STATE
    head_count = dt_raw.shape[0]
    per_group = head_count // group_count
    inputs = mamba_x.astype(jnp.float32).reshape(tokens_here, group_count, per_group, MHEAD_DIM)
    b_group = b_in.astype(jnp.float32).reshape(tokens_here, group_count, STATE)
    c_group = c_in.astype(jnp.float32).reshape(tokens_here, group_count, STATE)
    time_step = jax.nn.softplus(dt_raw).reshape(group_count, per_group, tokens_here)
    decay_rate = jnp.exp(a_log).reshape(group_count, per_group)
    log_decay, local_out, summary, totals = block_scan(
        inputs, b_group, c_group, time_step, decay_rate
    )
    state_in = carried_state(totals, summary)
    skip_heads = skip_d.reshape(group_count, per_group)[None, :, :, None]
    ssm_out = local_out + carried_out(c_group, state_in, log_decay) + skip_heads * inputs
    mamba_out = gated_norm(ssm_out.reshape(tokens_here, -1), gate_z, norm_gain, group_count)
    kv_here = keys.shape[1] // HEAD_DIM
    per_kv = QHEADS // KVHEADS
    tp_count = lax.axis_size("tp")
    product = jnp.dot(mamba_out, value_weight, preferred_element_type=jnp.float32)
    partials = jnp.transpose(
        product.reshape(tokens_here, tp_count, kv_here * HEAD_DIM), (1, 0, 2)
    )
    exchanged = lax.all_to_all(partials, "tp", 0, 0, tiled=True)
    values = jnp.sum(exchanged, axis=0).astype(jnp.bfloat16)
    values = jnp.transpose(values.reshape(tokens_here, kv_here, HEAD_DIM), (1, 0, 2))
    key_heads = jnp.transpose(keys.reshape(tokens_here, kv_here, HEAD_DIM), (1, 0, 2))
    pair = jnp.stack([key_heads, values])
    pair = gather_by_exchange(lax.all_gather(pair, ("zh", "zl")), "sx")
    all_pairs = jnp.transpose(pair, (2, 3, 1, 0, 4, 5)).reshape(2, kv_here, -1, HEAD_DIM)
    key_portion = all_pairs[0]
    value_portion = all_pairs[1]
    my_index = lax.axis_index(ROWS)
    query_block = query_layout(queries, kv_here, per_kv)
    query_pos = row_positions(my_index * tokens_here, tokens_here, per_kv)
    key_pos = jnp.arange(key_portion.shape[1], dtype=jnp.int32)
    scores = jnp.einsum(
        "hrd,hcd->hrc", query_block, key_portion, preferred_element_type=jnp.float32
    ) * (1.0 / math.sqrt(HEAD_DIM))
    allowed = key_pos[None, :] <= query_pos[:, None]
    scores = jnp.where(allowed[None], scores, -jnp.inf)
    row_max = jnp.max(scores, axis=2, keepdims=True)
    weights = jnp.exp(scores - row_max)
    total = jnp.sum(weights, axis=2)
    weighted = jnp.einsum(
        "hrc,hcd->hrd", weights.astype(jnp.bfloat16), value_portion, preferred_element_type=jnp.float32
    )
    attention = set_output((row_max, total, weighted), kv_here, per_kv)
    return (mamba_out, attention)


def solution(mesh):
    seq_count = mesh.shape["seq"]
    split = Mesh(
        mesh.devices.reshape(seq_count // 16, 4, 4, mesh.shape["tp"]),
        ROWS + ("tp",),
    )
    rows = ROWS
    placed = (
        P(rows, "tp"),
        P(rows, "tp"),
        P(rows, "tp"),
        P(rows, "tp"),
        P("tp", rows),
        P("tp"),
        P("tp"),
        P("tp"),
        P("tp", None),
        P(rows, "tp"),
        P(rows, "tp"),
    )
    return jax.shard_map(
        per_device,
        mesh=split,
        in_specs=placed,
        out_specs=(P(rows, "tp"), P(rows, "tp")),
        check_vma=False,
    )
```

```python
import math

import jax
import jax.numpy as jnp
from jax import lax
from jax.sharding import Mesh, PartitionSpec as P

MHEAD_DIM = 64
STATE = 128
QHEADS = 32
KVHEADS = 8
HEAD_DIM = 128
SEQ_AXES = (("zl", "sx"), "zh")
ROWS = ("zh", "zl", "sx")
TP = ("ty", "tc")


highest = lax.Precision.HIGHEST
norm_eps = 1e-05


def block_scan(inputs, b_group, c_group, time_step, decay_rate):
    token_count = inputs.shape[0]
    log_decay = jnp.cumsum(-time_step * decay_rate[..., None], axis=2)
    log_gaps = log_decay[..., :, None] - log_decay[..., None, :]
    causal = jnp.arange(token_count)[:, None] >= jnp.arange(token_count)[None, :]
    decay_mat = jnp.exp(jnp.where(causal, log_gaps, -jnp.inf))
    cross_terms = jnp.einsum("tgn,sgn->gts", c_group, b_group, precision=highest)
    mixing = cross_terms[:, None] * decay_mat * time_step[:, :, None, :]
    local_out = jnp.einsum("gkts,sgkp->tgkp", mixing, inputs, precision=highest)
    tail_weight = jnp.exp(log_decay[..., -1:] - log_decay) * time_step
    summary = jnp.einsum("gks,sgkp,sgn->gkpn", tail_weight, inputs, b_group, precision=highest)
    return (log_decay, local_out, summary, jnp.exp(log_decay[..., -1]))


def carried_out(c_group, state_in, log_decay):
    carried_term = jnp.einsum("tgn,gkpn->tgkp", c_group, state_in, precision=highest)
    return carried_term * jnp.transpose(jnp.exp(log_decay), (2, 0, 1))[..., None]


def gated_norm(ssm_out, gate_z, norm_gain, group_count):
    token_count = ssm_out.shape[0]
    gated = ssm_out * jax.nn.silu(gate_z.astype(jnp.float32))
    grouped = gated.reshape(token_count, group_count, -1)
    inverse = lax.rsqrt(jnp.mean(grouped * grouped, axis=2, keepdims=True) + norm_eps)
    return ((grouped * inverse).reshape(token_count, -1) * norm_gain).astype(jnp.bfloat16)


def query_layout(payload, kv_here, per_kv):
    count_rows = payload.shape[0]
    shaped = payload.reshape(count_rows, kv_here, per_kv, HEAD_DIM)
    return jnp.transpose(shaped, (1, 2, 0, 3)).reshape(kv_here, per_kv * count_rows, HEAD_DIM)


def row_positions(first_pos, count_rows, per_kv):
    return jnp.tile(first_pos + jnp.arange(count_rows, dtype=jnp.int32), per_kv)


def set_output(finished_set, kv_here, per_kv):
    running_max, running_sum, running_out = finished_set
    count_rows = running_sum.shape[1] // per_kv
    result = (running_out / running_sum[..., None]).astype(jnp.bfloat16)
    result = result.reshape(kv_here, per_kv, count_rows, HEAD_DIM)
    return jnp.transpose(result, (2, 0, 1, 3)).reshape(count_rows, kv_here * per_kv * HEAD_DIM)


def gather_by_exchange(block, axis):
    count = lax.axis_size(axis)
    repeated = jnp.broadcast_to(block[None], (count,) + block.shape)
    return lax.all_to_all(repeated, axis, 0, 0, tiled=True)


def masked_weights(decays, upto):
    count = decays.shape[0]
    earlier = jnp.arange(count)[:, None]
    later = jnp.arange(count)[None, :]
    between = (later > earlier) & (later < upto)
    spans = jnp.prod(jnp.where(between[:, :, None], decays[None, :, :], 1.0), axis=1)
    return jnp.where((jnp.arange(count) < upto)[:, None], spans, 0.0)


def pack_decay(state, decay):
    extra = jnp.broadcast_to(decay[..., None, None], decay.shape + (8, state.shape[-1]))
    return jnp.concatenate([state, extra], axis=-2)


def entering_top(axis, decay, state):
    rows = state.shape[-2]
    gathered = lax.all_gather(pack_decay(state, decay), axis)
    weights = masked_weights(gathered[:, :, rows, 0], lax.axis_index(axis))
    return jnp.sum(weights[:, :, None, None] * gathered[:, :, :rows], axis=0)


def entering_state(axes, decay, state):
    if len(axes) == 1:
        return entering_top(axes[0], decay, state)
    axis = axes[0]
    count = lax.axis_size(axis)
    head_total, rows, lanes = state.shape
    part = head_total // count
    packed = pack_decay(state.reshape(count, part, rows, lanes), decay.reshape(count, part))
    received = lax.all_to_all(packed, axis, 0, 0, tiled=True)
    decays = received[:, :, rows, 0]
    states = received[:, :, :rows]
    member = jnp.arange(count)
    bounds = jnp.arange(count + 1)
    earlier = member[None, :, None]
    between = (member[None, None, :] > member[None, :, None]) & (
        member[None, None, :] < bounds[:, None, None]
    )
    spans = jnp.prod(
        jnp.where(between[:, :, :, None], decays[None, None, :, :], 1.0), axis=2
    )
    weights = jnp.where(earlier < bounds[:, None, None], spans, 0.0)
    prefixes = jnp.sum(weights[:, :, :, None, None] * states[None], axis=1)
    decay_before = jnp.prod(
        jnp.where(earlier < bounds[:, None, None], decays[None], 1.0), axis=1
    )
    group_in = entering_state(axes[1:], decay_before[count], prefixes[count])
    outgoing = decay_before[:count, :, None, None] * group_in[None] + prefixes[:count]
    returned = lax.all_to_all(outgoing, axis, 0, 0, tiled=True)
    return returned.reshape(head_total, rows, lanes)


def carried_state(totals, summary):
    head_total = totals.size
    state_in = entering_state(
        SEQ_AXES, totals.reshape(head_total), summary.reshape((head_total,) + summary.shape[-2:])
    )
    return state_in.reshape(summary.shape)


def per_device(
    mamba_x, gate_z, b_in, c_in, dt_raw, a_log, skip_d, norm_gain, value_weight, queries, keys
):
    tokens_here = mamba_x.shape[0]
    group_count = b_in.shape[1] // STATE
    head_count = dt_raw.shape[0]
    per_group = head_count // group_count
    inputs = mamba_x.astype(jnp.float32).reshape(tokens_here, group_count, per_group, MHEAD_DIM)
    b_group = b_in.astype(jnp.float32).reshape(tokens_here, group_count, STATE)
    c_group = c_in.astype(jnp.float32).reshape(tokens_here, group_count, STATE)
    time_step = jax.nn.softplus(dt_raw).reshape(group_count, per_group, tokens_here)
    decay_rate = jnp.exp(a_log).reshape(group_count, per_group)
    log_decay, local_out, summary, totals = block_scan(
        inputs, b_group, c_group, time_step, decay_rate
    )
    state_in = carried_state(totals, summary)
    skip_heads = skip_d.reshape(group_count, per_group)[None, :, :, None]
    ssm_out = local_out + carried_out(c_group, state_in, log_decay) + skip_heads * inputs
    mamba_out = gated_norm(ssm_out.reshape(tokens_here, -1), gate_z, norm_gain, group_count)
    kv_here = keys.shape[1] // HEAD_DIM
    per_kv = QHEADS // KVHEADS
    chips = lax.axis_size("ty")
    cores = lax.axis_size("tc")
    product = jnp.dot(mamba_out, value_weight, preferred_element_type=jnp.float32)
    partials = jnp.transpose(
        product.reshape(tokens_here, chips, cores, kv_here * HEAD_DIM), (2, 1, 0, 3)
    )
    on_chip = jnp.sum(lax.all_to_all(partials, "tc", 0, 0, tiled=True), axis=0)
    values = jnp.sum(lax.all_to_all(on_chip, "ty", 0, 0, tiled=True), axis=0)
    values = values.astype(jnp.bfloat16)
    values = jnp.transpose(values.reshape(tokens_here, kv_here, HEAD_DIM), (1, 0, 2))
    key_heads = jnp.transpose(keys.reshape(tokens_here, kv_here, HEAD_DIM), (1, 0, 2))
    pair = jnp.stack([key_heads, values])
    pair = gather_by_exchange(lax.all_gather(pair, ("zh", "zl")), "sx")
    all_pairs = jnp.transpose(pair, (2, 3, 1, 0, 4, 5)).reshape(2, kv_here, -1, HEAD_DIM)
    key_portion = all_pairs[0]
    value_portion = all_pairs[1]
    my_index = lax.axis_index(ROWS)
    query_block = query_layout(queries, kv_here, per_kv)
    query_pos = row_positions(my_index * tokens_here, tokens_here, per_kv)
    key_pos = jnp.arange(key_portion.shape[1], dtype=jnp.int32)
    scores = jnp.einsum(
        "hrd,hcd->hrc", query_block, key_portion, preferred_element_type=jnp.float32
    ) * (1.0 / math.sqrt(HEAD_DIM))
    allowed = key_pos[None, :] <= query_pos[:, None]
    scores = jnp.where(allowed[None], scores, -jnp.inf)
    row_max = jnp.max(scores, axis=2, keepdims=True)
    weights = jnp.exp(scores - row_max)
    total = jnp.sum(weights, axis=2)
    weighted = jnp.einsum(
        "hrc,hcd->hrd", weights.astype(jnp.bfloat16), value_portion, preferred_element_type=jnp.float32
    )
    attention = set_output((row_max, total, weighted), kv_here, per_kv)
    return (mamba_out, attention)


def solution(mesh):
    seq_count = mesh.shape["seq"]
    split = Mesh(
        mesh.devices.reshape(seq_count // 16, 4, 4, mesh.shape["tp"] // 2, 2),
        ROWS + TP,
    )
    rows = ROWS
    placed = (
        P(rows, TP),
        P(rows, TP),
        P(rows, TP),
        P(rows, TP),
        P(TP, rows),
        P(TP),
        P(TP),
        P(TP),
        P(TP, None),
        P(rows, TP),
        P(rows, TP),
    )
    return jax.shard_map(
        per_device,
        mesh=split,
        in_specs=placed,
        out_specs=(P(rows, TP), P(rows, TP)),
        check_vma=False,
    )
```

```python
import math

import jax
import jax.numpy as jnp
from jax import lax
from jax.sharding import Mesh, PartitionSpec as P

MHEAD_DIM = 64
STATE = 128
QHEADS = 32
KVHEADS = 8
HEAD_DIM = 128
SEQ_AXES = (("zl", "sx"), "zh")
ROWS = ("zh", "zl", "sx")


highest = lax.Precision.HIGHEST
norm_eps = 1e-05


def block_scan(inputs, b_group, c_group, time_step, decay_rate):
    token_count = inputs.shape[0]
    log_decay = jnp.cumsum(-time_step * decay_rate[..., None], axis=2)
    log_gaps = log_decay[..., :, None] - log_decay[..., None, :]
    causal = jnp.arange(token_count)[:, None] >= jnp.arange(token_count)[None, :]
    decay_mat = jnp.exp(jnp.where(causal, log_gaps, -jnp.inf))
    cross_terms = jnp.einsum("tgn,sgn->gts", c_group, b_group, precision=highest)
    mixing = cross_terms[:, None] * decay_mat * time_step[:, :, None, :]
    local_out = jnp.einsum("gkts,sgkp->tgkp", mixing, inputs, precision=highest)
    tail_weight = jnp.exp(log_decay[..., -1:] - log_decay) * time_step
    summary = jnp.einsum("gks,sgkp,sgn->gkpn", tail_weight, inputs, b_group, precision=highest)
    return (log_decay, local_out, summary, jnp.exp(log_decay[..., -1]))


def carried_out(c_group, state_in, log_decay):
    carried_term = jnp.einsum("tgn,gkpn->tgkp", c_group, state_in, precision=highest)
    return carried_term * jnp.transpose(jnp.exp(log_decay), (2, 0, 1))[..., None]


def gated_norm(ssm_out, gate_z, norm_gain, group_count):
    token_count = ssm_out.shape[0]
    gated = ssm_out * jax.nn.silu(gate_z.astype(jnp.float32))
    grouped = gated.reshape(token_count, group_count, -1)
    inverse = lax.rsqrt(jnp.mean(grouped * grouped, axis=2, keepdims=True) + norm_eps)
    return ((grouped * inverse).reshape(token_count, -1) * norm_gain).astype(jnp.bfloat16)


def query_layout(payload, kv_here, per_kv):
    count_rows = payload.shape[0]
    shaped = payload.reshape(count_rows, kv_here, per_kv, HEAD_DIM)
    return jnp.transpose(shaped, (1, 2, 0, 3)).reshape(kv_here, per_kv * count_rows, HEAD_DIM)


def row_positions(first_pos, count_rows, per_kv):
    return jnp.tile(first_pos + jnp.arange(count_rows, dtype=jnp.int32), per_kv)


def set_output(finished_set, kv_here, per_kv):
    running_max, running_sum, running_out = finished_set
    count_rows = running_sum.shape[1] // per_kv
    result = (running_out / running_sum[..., None]).astype(jnp.bfloat16)
    result = result.reshape(kv_here, per_kv, count_rows, HEAD_DIM)
    return jnp.transpose(result, (2, 0, 1, 3)).reshape(count_rows, kv_here * per_kv * HEAD_DIM)


def gather_by_exchange(block, axis):
    count = lax.axis_size(axis)
    repeated = jnp.broadcast_to(block[None], (count,) + block.shape)
    return lax.all_to_all(repeated, axis, 0, 0, tiled=True)


def masked_weights(decays, upto):
    count = decays.shape[0]
    earlier = jnp.arange(count)[:, None]
    later = jnp.arange(count)[None, :]
    between = (later > earlier) & (later < upto)
    spans = jnp.prod(jnp.where(between[:, :, None], decays[None, :, :], 1.0), axis=1)
    return jnp.where((jnp.arange(count) < upto)[:, None], spans, 0.0)


def pack_decay(state, decay):
    extra = jnp.broadcast_to(decay[..., None, None], decay.shape + (8, state.shape[-1]))
    return jnp.concatenate([state, extra], axis=-2)


def entering_top(axis, decay, state):
    rows = state.shape[-2]
    gathered = lax.all_gather(pack_decay(state, decay), axis)
    weights = masked_weights(gathered[:, :, rows, 0], lax.axis_index(axis))
    return jnp.sum(weights[:, :, None, None] * gathered[:, :, :rows], axis=0)


def entering_state(axes, decay, state):
    if len(axes) == 1:
        return entering_top(axes[0], decay, state)
    axis = axes[0]
    count = lax.axis_size(axis)
    head_total, rows, lanes = state.shape
    part = head_total // count
    packed = pack_decay(state.reshape(count, part, rows, lanes), decay.reshape(count, part))
    received = lax.all_to_all(packed, axis, 0, 0, tiled=True)
    decays = received[:, :, rows, 0]
    states = received[:, :, :rows]
    member = jnp.arange(count)
    bounds = jnp.arange(count + 1)
    earlier = member[None, :, None]
    between = (member[None, None, :] > member[None, :, None]) & (
        member[None, None, :] < bounds[:, None, None]
    )
    spans = jnp.prod(
        jnp.where(between[:, :, :, None], decays[None, None, :, :], 1.0), axis=2
    )
    weights = jnp.where(earlier < bounds[:, None, None], spans, 0.0)
    prefixes = jnp.sum(weights[:, :, :, None, None] * states[None], axis=1)
    decay_before = jnp.prod(
        jnp.where(earlier < bounds[:, None, None], decays[None], 1.0), axis=1
    )
    group_in = entering_state(axes[1:], decay_before[count], prefixes[count])
    outgoing = decay_before[:count, :, None, None] * group_in[None] + prefixes[:count]
    returned = lax.all_to_all(outgoing, axis, 0, 0, tiled=True)
    return returned.reshape(head_total, rows, lanes)


def carried_state(totals, summary):
    head_total = totals.size
    state_in = entering_state(
        SEQ_AXES, totals.reshape(head_total), summary.reshape((head_total,) + summary.shape[-2:])
    )
    return state_in.reshape(summary.shape)


def per_device(
    mamba_x, gate_z, b_in, c_in, dt_raw, a_log, skip_d, norm_gain, value_weight, queries, keys
):
    tokens_here = mamba_x.shape[0]
    group_count = b_in.shape[1] // STATE
    head_count = dt_raw.shape[0]
    per_group = head_count // group_count
    inputs = mamba_x.astype(jnp.float32).reshape(tokens_here, group_count, per_group, MHEAD_DIM)
    b_group = b_in.astype(jnp.float32).reshape(tokens_here, group_count, STATE)
    c_group = c_in.astype(jnp.float32).reshape(tokens_here, group_count, STATE)
    time_step = jax.nn.softplus(dt_raw).reshape(group_count, per_group, tokens_here)
    decay_rate = jnp.exp(a_log).reshape(group_count, per_group)
    log_decay, local_out, summary, totals = block_scan(
        inputs, b_group, c_group, time_step, decay_rate
    )
    state_in = carried_state(totals, summary)
    skip_heads = skip_d.reshape(group_count, per_group)[None, :, :, None]
    ssm_out = local_out + carried_out(c_group, state_in, log_decay) + skip_heads * inputs
    mamba_out = gated_norm(ssm_out.reshape(tokens_here, -1), gate_z, norm_gain, group_count)
    kv_here = keys.shape[1] // HEAD_DIM
    per_kv = QHEADS // KVHEADS
    tp_count = lax.axis_size("tp")
    product = jnp.dot(mamba_out, value_weight, preferred_element_type=jnp.float32)
    partials = jnp.transpose(
        product.reshape(tokens_here, tp_count, kv_here * HEAD_DIM), (1, 0, 2)
    )
    exchanged = lax.all_to_all(partials, "tp", 0, 0, tiled=True)
    values = jnp.sum(exchanged, axis=0).astype(jnp.bfloat16)
    values = jnp.transpose(values.reshape(tokens_here, kv_here, HEAD_DIM), (1, 0, 2))
    key_heads = jnp.transpose(keys.reshape(tokens_here, kv_here, HEAD_DIM), (1, 0, 2))
    pair = jnp.stack([key_heads, values])
    pair = lax.all_gather(pair, ("zh", "zl"))
    key_portion, value_portion = (
        jnp.transpose(gather_by_exchange(pair[:, part], "sx"), (2, 1, 0, 3, 4)).reshape(
            kv_here, -1, HEAD_DIM
        )
        for part in range(2)
    )
    my_index = lax.axis_index(ROWS)
    query_block = query_layout(queries, kv_here, per_kv)
    query_pos = row_positions(my_index * tokens_here, tokens_here, per_kv)
    key_pos = jnp.arange(key_portion.shape[1], dtype=jnp.int32)
    scores = jnp.einsum(
        "hrd,hcd->hrc", query_block, key_portion, preferred_element_type=jnp.float32
    ) * (1.0 / math.sqrt(HEAD_DIM))
    allowed = key_pos[None, :] <= query_pos[:, None]
    scores = jnp.where(allowed[None], scores, -jnp.inf)
    row_max = jnp.max(scores, axis=2, keepdims=True)
    weights = jnp.exp(scores - row_max)
    total = jnp.sum(weights, axis=2)
    weighted = jnp.einsum(
        "hrc,hcd->hrd", weights.astype(jnp.bfloat16), value_portion, preferred_element_type=jnp.float32
    )
    attention = set_output((row_max, total, weighted), kv_here, per_kv)
    return (mamba_out, attention)


def solution(mesh):
    seq_count = mesh.shape["seq"]
    split = Mesh(
        mesh.devices.reshape(seq_count // 16, 4, 4, mesh.shape["tp"]),
        ROWS + ("tp",),
    )
    rows = ROWS
    placed = (
        P(rows, "tp"),
        P(rows, "tp"),
        P(rows, "tp"),
        P(rows, "tp"),
        P("tp", rows),
        P("tp"),
        P("tp"),
        P("tp"),
        P("tp", None),
        P(rows, "tp"),
        P(rows, "tp"),
    )
    return jax.shard_map(
        per_device,
        mesh=split,
        in_specs=placed,
        out_specs=(P(rows, "tp"), P(rows, "tp")),
        check_vma=False,
    )
```
